512 devices in a mesh: ctx: 32 (over z_hi, y, x), exp: 16 (over z_lo, core).
Axes of the slice: x: 4, y: 4, z: 16 (z_hi: 2, z_lo: 8; z = z_hi * 8 + z_lo), core: 2. Of those that a mesh axis runs over, the one named last changes fastest.
Arguments:
- hidden_in: bfloat16 [4096, 2880], P('ctx'), may hold values from -6 to 6
- query_input: bfloat16 [4096, 2048], P('ctx', 'exp'), may hold values from -16 to 16
- key_heads_input: bfloat16 [4096, 256], P('ctx'), may hold values from -16 to 16
- value_heads_input: bfloat16 [4096, 256], P('ctx'), may hold values from -6 to 6
- sink_logits: float32 [32], P('exp'), may hold values from 0 to 4
- out_proj: bfloat16 [2048, 2880], P('exp'), may hold values from -0.125 to 0.125
- norm_gain: float32 [2880], replicated, may hold values from 0.5 to 1.5
- expert_ids: int32 [4096, 4], P('ctx'), may hold values from 0 to 31, all different within a row; in each aligned block of 128 rows (0 to 127, 128 to 255, ...) at most 20 rows name the same one
- expert_gates: float32 [4096, 4], P('ctx'), may hold values from 0.1 to 1
- gate_up: bfloat16 [32, 2880, 2, 2880], P('ctx', None, None, 'exp'), may hold values from -0.109375 to 0.109375
- down_proj: bfloat16 [32, 2880, 2880], P('ctx', 'exp'), may hold values from -0.109375 to 0.109375
Outputs:
- layer_out: bfloat16 [4096, 2880], P('ctx', 'exp')
The draws below stay inside these ranges and needn't reach their ends.
Inputs may be any that keep to these rules, and one draw needn't show every extreme that they name: `expert_ids`: each token names 4 different experts; within the 128 tokens of one device no expert is named by more than 20 tokens.
All inputs are finite; a program needn't handle non-finite values.
Results may differ from the reference program's by a relative error of at most 0.02.
Values may be sent and summed in bfloat16 or wider, within the bound.
No kernel may reach another device: no remote copies, remote signals or barrier semaphores. Data moves between devices by JAX's collectives and lax.ppermute only.
A program may use at most 64 MiB of HBM per device.

```python
import math
import jax
import jax.numpy as jnp
import numpy as np
from jax import lax

D = 2880
QUERY_HEADS = 32
KEY_VALUE_HEADS = 4
HEAD_SIZE = 64
FF = 2880
TOPK = 4
BLOCK_TOKENS = 128
SEQUENCE_TOKENS = 4096
EXPERTS = 32
CAP = 20
N_CTX = 32
N_EXP = 16


def outlier_rows(key, row_count, col_count):
    base = jax.random.normal(jax.random.fold_in(key, 1), (row_count, col_count), jnp.float32)
    return jnp.clip(base, -16.0, 16.0)


def draw_query_input(key, part):
    return outlier_rows(jax.random.fold_in(key, 11), BLOCK_TOKENS * N_CTX, QUERY_HEADS * HEAD_SIZE).astype(jnp.bfloat16)


def draw_key_heads_input(key, part):
    return outlier_rows(jax.random.fold_in(key, 23), BLOCK_TOKENS * N_CTX, KEY_VALUE_HEADS * HEAD_SIZE).astype(jnp.bfloat16)


def block_levels(key, extent, split, least, high):
    level, own = 1.0, jax.random.fold_in(key, 6)
    for axis_at, parts in split:
        draws = jnp.exp(jax.random.uniform(jax.random.fold_in(own, axis_at), (parts,), jnp.float32, least / len(split), high / len(split)))
        level = level * jnp.repeat(draws, extent[axis_at] // parts).reshape([-1 if axis == axis_at else 1 for axis in range(len(extent))])
    return level


def routed_block(key, own, number, rows, amount, top, most, lean):
    sequence = jax.random.permutation(key, amount)
    heavy_load, common = shares(amount, rows * top, most, lean, True), shares(amount, rows * top, most, lean, False)
    places = jnp.arange(amount)

    def named(tallies, turn):
        used = int((tallies > 0).sum())
        fixed = max(1, used // 4)
        shifted = fixed + (places - fixed + turn * (used - fixed)) % max(1, amount - fixed)
        return jnp.zeros((amount,), jnp.int32).at[sequence[jnp.where(places < fixed, places, shifted)]].set(jnp.asarray(tallies, jnp.int32))

    tallies = jnp.where(number % 4 == 0, named(heavy_load, number // 4), named(common, number - number // 4 - 1))
    mixed = jax.random.permutation(jax.random.fold_in(own, 3), amount)
    source_of, taker = mixed[0:amount // 2 * 2:2], mixed[1:amount // 2 * 2:2]
    slack = jnp.minimum(tallies[source_of] - 1, most - tallies[taker]) // 2
    slack = jnp.where((source_of == sequence[0]) | (taker == sequence[0]) | (tallies[taker] == 0), 0, jnp.maximum(slack, 0))
    shifted = jax.random.randint(jax.random.fold_in(own, 4), (amount // 2,), 0, 1 << 20) % (slack + 1)
    tallies = tallies.at[source_of].add(-shifted).at[taker].add(shifted)
    items = jnp.searchsorted(jnp.cumsum(tallies), jnp.arange(rows * top), side="right").astype(jnp.int32)
    listing = items.reshape(top, rows).T
    listing = listing[jax.random.permutation(jax.random.fold_in(own, 1), rows)]
    turn = jax.random.randint(jax.random.fold_in(own, 2), (rows, 1), 0, top)
    return jnp.take_along_axis(listing, (jnp.arange(top)[None, :] + turn) % top, axis=1)


def shares(amount, total, limit, slope, full):
    portions = [(1 << 20) // math.isqrt(rank ** slope) + 1 for rank in range(1, amount + 1)]
    largest = limit if full else min(limit, max(-(-total // amount), total * portions[0] // sum(portions)))
    least = 1 if total - largest >= amount - 1 else 0
    counts, rest = [largest] + [least] * (amount - 1), total - largest - least * (amount - 1)
    while rest > 0:
        movable = [i for i in range(1, amount) if counts[i] < largest] or [i for i in range(1, amount) if counts[i] < limit]
        pool, remaining = sum([portions[i] for i in movable]), rest
        for i in movable:
            more = min(limit - counts[i], max(1, remaining * portions[i] // pool), rest)
            counts[i] = counts[i] + more
            rest = rest - more
    return np.array(counts)


def gaussian(stream_key, dims, width, reach, shards=(), kind=jnp.bfloat16):
    array = jax.random.normal(stream_key, dims, jnp.float32) * width
    if len(shards) > 0:
        array = block_levels(stream_key, dims, shards, -0.22, 0.18) * array
    return jnp.clip(array, min=-reach, max=reach).astype(kind)


def setup_inputs(seed: int = 0) -> dict:
    streams_of = jax.random.split(jax.random.key(seed), 12)
    hidden_in = gaussian(streams_of[0], (SEQUENCE_TOKENS, D), 1.0, 6.0, ((0, 32),))
    query_input = draw_query_input(jax.random.fold_in(streams_of[11], 71), 0)
    key_heads_input = draw_key_heads_input(jax.random.fold_in(streams_of[11], 71), 0)
    value_heads_input = gaussian(streams_of[3], (SEQUENCE_TOKENS, KEY_VALUE_HEADS * HEAD_SIZE), 1.0, 6.0, ((0, 32),))
    sink_logits = jnp.clip(4.0 * jax.random.uniform(streams_of[4], (QUERY_HEADS,), jnp.float32) ** block_levels(streams_of[4], (QUERY_HEADS,), ((0, 16),), -0.2, 0.2), 0.0, 4.0)
    out_proj = gaussian(streams_of[5], (QUERY_HEADS * HEAD_SIZE, D), (QUERY_HEADS * HEAD_SIZE) ** -0.5, 0.125, ((0, 16),))
    norm_gain = jnp.clip(1.0 + 0.1 * jax.random.normal(streams_of[6], (D,), jnp.float32), 0.5, 1.5)
    expert_ids_keys = jax.random.split(jax.random.fold_in(streams_of[7], 1), SEQUENCE_TOKENS // BLOCK_TOKENS)
    expert_ids_turns = jax.random.permutation(jax.random.fold_in(streams_of[7], 3), SEQUENCE_TOKENS // BLOCK_TOKENS)
    expert_ids = jax.vmap(lambda own, number: routed_block(jax.random.fold_in(streams_of[7], 2), own, number, BLOCK_TOKENS, EXPERTS, TOPK, CAP, 1))(expert_ids_keys, expert_ids_turns).reshape((SEQUENCE_TOKENS, TOPK))
    expert_gates = jnp.clip(0.1 + 0.9 * jax.random.uniform(streams_of[8], (SEQUENCE_TOKENS, TOPK), jnp.float32) ** block_levels(streams_of[8], (SEQUENCE_TOKENS, TOPK), ((0, 32),), -0.2, 0.2), 0.1, 1.0)
    gate_up = gaussian(streams_of[9], (EXPERTS, D, 2, FF), D ** -0.5, 0.109375, ((0, 32), (3, 16)))
    down_proj = gaussian(streams_of[10], (EXPERTS, FF, D), FF ** -0.5, 0.109375, ((0, 32), (1, 16)))
    return dict(hidden_in=hidden_in, query_input=query_input, key_heads_input=key_heads_input, value_heads_input=value_heads_input, sink_logits=sink_logits, out_proj=out_proj, norm_gain=norm_gain, expert_ids=expert_ids, expert_gates=expert_gates, gate_up=gate_up, down_proj=down_proj)


yarn_base = 150000.0
yarn_factor = 32.0
yarn_initial = 4096.0
beta_fast = 32.0
beta_slow = 1.0
neg_large = -1e+30

def yarn_frequencies(head_dim):
    half_dim = head_dim // 2

    def correction(rotations):
        return head_dim * math.log(yarn_initial / (rotations * 2.0 * math.pi)) / (2.0 * math.log(yarn_base))
    lower_dim = max(math.floor(correction(beta_fast)), 0)
    upper_dim = min(math.ceil(correction(beta_slow)), head_dim - 1)
    extrap_freq = 1.0 / yarn_base ** (np.arange(0, head_dim, 2) / head_dim)
    interp_freq = extrap_freq / yarn_factor
    ramp_part = np.clip((np.arange(half_dim) - lower_dim) / (upper_dim - lower_dim), 0.0, 1.0)
    extrap_share = 1.0 - ramp_part
    return (interp_freq * (1.0 - extrap_share) + extrap_freq * extrap_share).astype(np.float32)

def rotate_with_yarn(heads_in, token_positions):
    head_dim = heads_in.shape[-1]
    freqs = jnp.asarray(yarn_frequencies(head_dim))
    angles = token_positions.astype(jnp.float32)[:, None] * freqs[None, :]
    factor = 0.1 * math.log(yarn_factor) + 1.0
    cosine = (jnp.cos(angles) * factor)[:, None, :]
    sine = (jnp.sin(angles) * factor)[:, None, :]
    first_half = heads_in[..., :head_dim // 2]
    second_half = heads_in[..., head_dim // 2:]
    return jnp.concatenate([first_half * cosine - second_half * sine, second_half * cosine + first_half * sine], axis=-1)

def route_slots(ids_block, n_experts):
    flat_ids = ids_block.reshape(-1)
    onehot = (flat_ids[:, None] == jnp.arange(n_experts, dtype=jnp.int32)[None, :]).astype(jnp.int32)
    ranks = jnp.cumsum(onehot, axis=0) - onehot
    return lax.optimization_barrier(jnp.sum(ranks * onehot, axis=1)).astype(jnp.int32).reshape(ids_block.shape)

def reference(hidden_in, query_input, key_heads_input, value_heads_input, sink_logits, out_proj, norm_gain, expert_ids, expert_gates, gate_up, down_proj):
    sequence_length = hidden_in.shape[0]
    token_positions = jnp.arange(sequence_length, dtype=jnp.int32)
    q_rot = rotate_with_yarn(query_input.astype(jnp.float32).reshape(sequence_length, QUERY_HEADS, HEAD_SIZE), token_positions).astype(jnp.bfloat16)
    rotated_keys = rotate_with_yarn(key_heads_input.astype(jnp.float32).reshape(sequence_length, KEY_VALUE_HEADS, HEAD_SIZE), token_positions).astype(jnp.bfloat16)
    value_heads = value_heads_input.reshape(sequence_length, KEY_VALUE_HEADS, HEAD_SIZE)
    query_group_width = QUERY_HEADS // KEY_VALUE_HEADS
    causal = token_positions[:, None] >= token_positions[None, :]
    score_scale = 1.0 / math.sqrt(HEAD_SIZE)

    def one_head(head):
        shared_key_head = head // query_group_width
        q_head = lax.dynamic_index_in_dim(q_rot, head, 1, keepdims=False)
        k_head = lax.dynamic_index_in_dim(rotated_keys, shared_key_head, 1, keepdims=False)
        v_head = lax.dynamic_index_in_dim(value_heads, shared_key_head, 1, keepdims=False).astype(jnp.float32)
        scores = jnp.dot(q_head, k_head.T, preferred_element_type=jnp.float32) * score_scale
        scores = jnp.where(causal, scores, neg_large)
        sink_value = sink_logits[head]
        row_max = jnp.maximum(lax.optimization_barrier(jnp.max(scores, axis=1)), sink_value)
        weights = jnp.exp(scores - row_max[:, None])
        row_total = lax.optimization_barrier(jnp.sum(weights, axis=1)) + jnp.exp(sink_value - row_max)
        return jnp.dot(weights, v_head, precision=lax.Precision.HIGHEST) / row_total[:, None]
    attended = lax.map(one_head, jnp.arange(QUERY_HEADS, dtype=jnp.int32))
    attended = attended.transpose(1, 0, 2).reshape(sequence_length, QUERY_HEADS * HEAD_SIZE).astype(jnp.bfloat16)
    residual = hidden_in.astype(jnp.float32) + jnp.dot(attended, out_proj, preferred_element_type=jnp.float32)
    mean_square = lax.optimization_barrier(jnp.mean(residual * residual, axis=1, keepdims=True))
    normed = (residual * lax.rsqrt(mean_square + 1e-05) * norm_gain[None, :]).astype(jnp.bfloat16)
    blocks = sequence_length // BLOCK_TOKENS
    slot_index = jax.vmap(lambda ids_block: route_slots(ids_block, EXPERTS))(expert_ids.reshape(blocks, BLOCK_TOKENS, TOPK))
    slot_index = slot_index.reshape(sequence_length, TOPK)
    block_of = (token_positions // BLOCK_TOKENS).astype(jnp.int32)[:, None]
    row_index = block_of * CAP + slot_index
    bucket_rows = blocks * CAP
    spread_rows = jnp.broadcast_to(normed[:, None, :], (sequence_length, TOPK, D))
    expert_rows = jnp.zeros((EXPERTS, bucket_rows, D), jnp.bfloat16).at[expert_ids, row_index].set(spread_rows)

    def one_expert(operands):
        rows_in, weights_gu, weights_down = operands
        gate_up_out = jnp.dot(rows_in, weights_gu.reshape(D, 2 * FF), preferred_element_type=jnp.float32).reshape(bucket_rows, 2, FF)
        gate_value = gate_up_out[:, 0]
        up_value = gate_up_out[:, 1]
        activated = ((up_value + 1.0) * gate_value * jax.nn.sigmoid(1.702 * gate_value)).astype(jnp.bfloat16)
        groups = activated.reshape(bucket_rows, N_EXP, FF // N_EXP).astype(jnp.float32)
        down_groups = weights_down.reshape(N_EXP, FF // N_EXP, D).astype(jnp.float32)
        partial_value = jnp.einsum('rsf,sfd->srd', groups, down_groups, precision=lax.Precision.HIGHEST)
        rounded = lax.optimization_barrier(partial_value.astype(jnp.bfloat16))
        return lax.optimization_barrier(jnp.sum(rounded.astype(jnp.float32), axis=0))
    expert_out = lax.map(one_expert, (expert_rows, gate_up, down_proj))
    picked_rows = expert_out[expert_ids, row_index]
    moe = lax.optimization_barrier(jnp.sum(expert_gates[:, :, None] * picked_rows, axis=1))
    return (residual + moe).astype(jnp.bfloat16)
```

```python
import functools
import math

import jax
import jax.numpy as jnp
import numpy as np
from jax import lax
from jax.sharding import Mesh, PartitionSpec as P

D = 2880
QUERY_HEADS = 32
KEY_VALUE_HEADS = 4
HEAD_SIZE = 64


yarn_base = 150000.0
yarn_factor = 32.0
yarn_initial = 4096.0
beta_fast = 32.0
beta_slow = 1.0
neg_large = -1e30


def yarn_frequencies(head_dim):
    half_dim = head_dim // 2

    def correction(rotations):
        return (
            head_dim
            * math.log(yarn_initial / (rotations * 2.0 * math.pi))
            / (2.0 * math.log(yarn_base))
        )

    lower_dim = max(math.floor(correction(beta_fast)), 0)
    upper_dim = min(math.ceil(correction(beta_slow)), head_dim - 1)
    extrap_freq = 1.0 / yarn_base ** (np.arange(0, head_dim, 2) / head_dim)
    interp_freq = extrap_freq / yarn_factor
    ramp_part = np.clip((np.arange(half_dim) - lower_dim) / (upper_dim - lower_dim), 0.0, 1.0)
    extrap_share = 1.0 - ramp_part
    return (interp_freq * (1.0 - extrap_share) + extrap_freq * extrap_share).astype(np.float32)


def rotate_with_yarn(heads_in, token_positions):
    head_dim = heads_in.shape[-1]
    freqs = jnp.asarray(yarn_frequencies(head_dim))
    angles = token_positions.astype(jnp.float32)[:, None] * freqs[None, :]
    factor = 0.1 * math.log(yarn_factor) + 1.0
    cosine = (jnp.cos(angles) * factor)[:, None, :]
    sine = (jnp.sin(angles) * factor)[:, None, :]
    first_half = heads_in[..., : head_dim // 2]
    second_half = heads_in[..., head_dim // 2 :]
    return jnp.concatenate(
        [first_half * cosine - second_half * sine, second_half * cosine + first_half * sine],
        axis=-1,
    )


def route_slots(ids_block, n_experts):
    flat_ids = ids_block.reshape(-1)
    onehot = (flat_ids[:, None] == jnp.arange(n_experts, dtype=jnp.int32)[None, :]).astype(
        jnp.int32
    )
    ranks = jnp.cumsum(onehot, axis=0) - onehot
    return jnp.sum(ranks * onehot, axis=1).reshape(ids_block.shape)


CTX = ("zh", "y", "x")
EXP = ("zl", "c")


def per_device(
    hidden_in,
    query_input,
    key_heads_input,
    value_heads_input,
    sink_logits,
    out_proj,
    norm_gain,
    expert_ids,
    expert_gates,
    gate_up,
    down_proj,
    *,
    ctx_count,
    zl_count,
    c_count,
):
    tok_rows = hidden_in.shape[0]
    exp_count = zl_count * c_count
    local_heads = query_input.shape[1] // HEAD_SIZE
    ctx_index = lax.axis_index(CTX)
    exp_index = lax.axis_index(EXP)
    token_positions = ctx_index * tok_rows + jnp.arange(tok_rows, dtype=jnp.int32)
    q_rot = rotate_with_yarn(
        query_input.astype(jnp.float32).reshape(tok_rows, local_heads, HEAD_SIZE), token_positions
    ).astype(jnp.bfloat16)
    shared_key_head = exp_index * local_heads // (QUERY_HEADS // KEY_VALUE_HEADS)
    key_block = lax.dynamic_slice_in_dim(key_heads_input, shared_key_head * HEAD_SIZE, HEAD_SIZE, 1)
    value_block = lax.dynamic_slice_in_dim(
        value_heads_input, shared_key_head * HEAD_SIZE, HEAD_SIZE, 1
    )
    key_rot = (
        rotate_with_yarn(
            key_block.astype(jnp.float32).reshape(tok_rows, 1, HEAD_SIZE), token_positions
        )
        .reshape(tok_rows, HEAD_SIZE)
        .astype(jnp.bfloat16)
    )
    key_value = jnp.concatenate([key_rot, value_block], axis=1)
    score_scale = 1.0 / math.sqrt(HEAD_SIZE)
    block_part = lax.all_gather(key_value, CTX, axis=0, tiled=True)
    run_max = jnp.broadcast_to(sink_logits[:, None], (local_heads, tok_rows))
    run_total = jnp.ones((local_heads, tok_rows), jnp.float32)
    key_count = block_part.shape[0]
    key_part = block_part[:, :HEAD_SIZE]
    value_part = block_part[:, HEAD_SIZE:].astype(jnp.float32)
    scores = (
        jnp.einsum("rhd,kd->hrk", q_rot, key_part, preferred_element_type=jnp.float32) * score_scale
    )
    key_pos = jnp.arange(key_count, dtype=jnp.int32)
    visible = token_positions[:, None] >= key_pos[None, :]
    scores = jnp.where(visible[None, :, :], scores, neg_large)
    new_max = jnp.maximum(run_max, jnp.max(scores, axis=2))
    weights = jnp.exp(scores - new_max[:, :, None])
    factor = jnp.exp(run_max - new_max)
    run_total = run_total * factor + jnp.sum(weights, axis=2)
    run_sum = jnp.einsum("hrk,kd->hrd", weights, value_part, precision=lax.Precision.HIGHEST)
    attended = (
        (run_sum / run_total[:, :, None])
        .transpose(1, 0, 2)
        .reshape(tok_rows, local_heads * HEAD_SIZE)
        .astype(jnp.bfloat16)
    )
    col_width = D // exp_count
    head_part = jnp.dot(attended, out_proj, preferred_element_type=jnp.float32).astype(jnp.bfloat16)
    head_part = head_part.reshape(tok_rows, zl_count, c_count, col_width).transpose(2, 1, 0, 3)
    head_part = lax.psum_scatter(head_part, "c", scatter_dimension=0, tiled=True)[0]
    head_cols = lax.psum_scatter(head_part, "zl", scatter_dimension=0, tiled=True)[0]
    residual_cols = lax.dynamic_slice_in_dim(
        hidden_in, exp_index * col_width, col_width, 1
    ).astype(jnp.float32) + head_cols.astype(jnp.float32)
    square_sum = lax.psum(jnp.sum(residual_cols * residual_cols, axis=1), EXP)
    gain_cols = lax.dynamic_slice_in_dim(norm_gain, exp_index * col_width, col_width, 0)
    normed_cols = (
        residual_cols * lax.rsqrt(square_sum / D + 1e-05)[:, None] * gain_cols[None, :]
    ).astype(jnp.bfloat16)
    exp_local = gate_up.shape[0]
    n_experts = exp_local * ctx_count
    top_count = expert_ids.shape[1]
    capacity = max(2, tok_rows * top_count * 5 // (4 * n_experts))
    slot_index = route_slots(expert_ids, n_experts)
    dest_row = expert_ids * capacity + slot_index
    spread_rows = jnp.broadcast_to(
        normed_cols[:, None, :], (tok_rows, top_count, col_width)
    ).reshape(tok_rows * top_count, col_width)
    send_rows = (
        jnp.zeros((n_experts * capacity, col_width), jnp.bfloat16)
        .at[dest_row.reshape(-1)]
        .set(spread_rows)
    )
    bucket_rows = ctx_count * capacity
    unit_count = gate_up.shape[-1]
    received = lax.all_to_all(
        send_rows.reshape(ctx_count, exp_local * capacity, col_width),
        CTX,
        split_axis=0,
        concat_axis=0,
        tiled=True,
    ).reshape(bucket_rows, col_width)
    gathered = lax.all_gather(received, "zl", axis=0, tiled=False)
    gathered = lax.all_gather(gathered, "c", axis=0, tiled=False)
    weights_flat = gate_up.reshape(zl_count, c_count, col_width, 2 * unit_count)
    gate_up_out = jnp.einsum(
        "czrk,zckf->rf", gathered, weights_flat, preferred_element_type=jnp.float32
    )
    gate_up_out = gate_up_out.reshape(bucket_rows, 2, unit_count)
    gate_value = gate_up_out[:, 0]
    up_value = gate_up_out[:, 1]
    activated = ((up_value + 1.0) * gate_value * jax.nn.sigmoid(1.702 * gate_value)).astype(
        jnp.bfloat16
    )
    down_local = down_proj.reshape(unit_count, zl_count, c_count, col_width)
    partial_value = jnp.einsum(
        "rf,fzcd->czrd", activated, down_local, preferred_element_type=jnp.float32
    ).astype(jnp.bfloat16)
    partial_value = lax.psum_scatter(partial_value, "c", scatter_dimension=0, tiled=True)[0]
    expert_cols = lax.psum_scatter(partial_value, "zl", scatter_dimension=0, tiled=True)[0]
    returned = lax.all_to_all(
        expert_cols.reshape(ctx_count, capacity, col_width),
        CTX,
        split_axis=0,
        concat_axis=0,
        tiled=True,
    )
    picked_rows = returned.reshape(n_experts * capacity, col_width)[dest_row]
    moe_cols = jnp.sum(expert_gates[:, :, None] * picked_rows.astype(jnp.float32), axis=1)
    return (residual_cols + moe_cols).astype(jnp.bfloat16)


def solution(mesh):
    ctx_count, exp_count = mesh.devices.shape
    zh, y, x = (mesh.devices.shape[0] // 16, 4, 4)
    c_count = 2
    zl_count = exp_count // c_count
    fine = Mesh(mesh.devices.reshape(zh, y, x, zl_count, c_count), ("zh", "y", "x", "zl", "c"))
    placed = (
        P(CTX, None),
        P(CTX, EXP),
        P(CTX, None),
        P(CTX, None),
        P(EXP),
        P(EXP, None),
        P(),
        P(CTX, None),
        P(CTX, None),
        P(CTX, None, None, EXP),
        P(CTX, EXP, None),
    )
    return jax.shard_map(
        functools.partial(per_device, ctx_count=ctx_count, zl_count=zl_count, c_count=c_count),
        mesh=fine,
        in_specs=placed,
        out_specs=P(CTX, EXP),
        check_vma=False,
    )
```

```python
import functools
import math

import jax
import jax.numpy as jnp
import numpy as np
from jax import lax
from jax.sharding import Mesh, PartitionSpec as P

D = 2880
QUERY_HEADS = 32
KEY_VALUE_HEADS = 4
HEAD_SIZE = 64


yarn_base = 150000.0
yarn_factor = 32.0
yarn_initial = 4096.0
beta_fast = 32.0
beta_slow = 1.0
neg_large = -1e30


def yarn_frequencies(head_dim):
    half_dim = head_dim // 2

    def correction(rotations):
        return (
            head_dim
            * math.log(yarn_initial / (rotations * 2.0 * math.pi))
            / (2.0 * math.log(yarn_base))
        )

    lower_dim = max(math.floor(correction(beta_fast)), 0)
    upper_dim = min(math.ceil(correction(beta_slow)), head_dim - 1)
    extrap_freq = 1.0 / yarn_base ** (np.arange(0, head_dim, 2) / head_dim)
    interp_freq = extrap_freq / yarn_factor
    ramp_part = np.clip((np.arange(half_dim) - lower_dim) / (upper_dim - lower_dim), 0.0, 1.0)
    extrap_share = 1.0 - ramp_part
    return (interp_freq * (1.0 - extrap_share) + extrap_freq * extrap_share).astype(np.float32)


def rotate_with_yarn(heads_in, token_positions):
    head_dim = heads_in.shape[-1]
    freqs = jnp.asarray(yarn_frequencies(head_dim))
    angles = token_positions.astype(jnp.float32)[:, None] * freqs[None, :]
    factor = 0.1 * math.log(yarn_factor) + 1.0
    cosine = (jnp.cos(angles) * factor)[:, None, :]
    sine = (jnp.sin(angles) * factor)[:, None, :]
    first_half = heads_in[..., : head_dim // 2]
    second_half = heads_in[..., head_dim // 2 :]
    return jnp.concatenate(
        [first_half * cosine - second_half * sine, second_half * cosine + first_half * sine],
        axis=-1,
    )


def route_slots(ids_block, n_experts):
    flat_ids = ids_block.reshape(-1)
    onehot = (flat_ids[:, None] == jnp.arange(n_experts, dtype=jnp.int32)[None, :]).astype(
        jnp.int32
    )
    ranks = jnp.cumsum(onehot, axis=0) - onehot
    return jnp.sum(ranks * onehot, axis=1).reshape(ids_block.shape)


CTX = ("zh", "y", "x")
EXP = ("zl", "c")


def per_device(
    hidden_in,
    query_input,
    key_heads_input,
    value_heads_input,
    sink_logits,
    out_proj,
    norm_gain,
    expert_ids,
    expert_gates,
    gate_up,
    down_proj,
    *,
    ctx_count,
    zl_count,
    c_count,
):
    tok_rows = hidden_in.shape[0]
    exp_count = zl_count * c_count
    local_heads = query_input.shape[1] // HEAD_SIZE
    ctx_index = lax.axis_index(CTX)
    exp_index = lax.axis_index(EXP)
    token_positions = ctx_index * tok_rows + jnp.arange(tok_rows, dtype=jnp.int32)
    q_rot = rotate_with_yarn(
        query_input.astype(jnp.float32).reshape(tok_rows, local_heads, HEAD_SIZE), token_positions
    ).astype(jnp.bfloat16)
    shared_key_head = exp_index * local_heads // (QUERY_HEADS // KEY_VALUE_HEADS)
    key_block = lax.dynamic_slice_in_dim(key_heads_input, shared_key_head * HEAD_SIZE, HEAD_SIZE, 1)
    value_block = lax.dynamic_slice_in_dim(
        value_heads_input, shared_key_head * HEAD_SIZE, HEAD_SIZE, 1
    )
    key_rot = (
        rotate_with_yarn(
            key_block.astype(jnp.float32).reshape(tok_rows, 1, HEAD_SIZE), token_positions
        )
        .reshape(tok_rows, HEAD_SIZE)
        .astype(jnp.bfloat16)
    )
    key_value = jnp.concatenate([key_rot, value_block], axis=1)
    score_scale = 1.0 / math.sqrt(HEAD_SIZE)
    block_part = lax.all_gather(key_value, "zh", axis=0, tiled=False)
    block_part = lax.all_gather(block_part, "y", axis=0, tiled=False)
    block_part = lax.all_gather(block_part, "x", axis=0, tiled=False)
    zh_count = block_part.shape[2]
    y_count = block_part.shape[1]
    x_count = block_part.shape[0]
    block_of_key = (
        lax.broadcasted_iota(jnp.int32, (x_count, y_count, zh_count), 2) * (y_count * x_count)
        + lax.broadcasted_iota(jnp.int32, (x_count, y_count, zh_count), 1) * x_count
        + lax.broadcasted_iota(jnp.int32, (x_count, y_count, zh_count), 0)
    )
    key_pos = (
        block_of_key[:, :, :, None] * tok_rows + jnp.arange(tok_rows, dtype=jnp.int32)
    ).reshape(-1)
    block_part = block_part.reshape(-1, 2 * HEAD_SIZE)
    run_max = jnp.broadcast_to(sink_logits[:, None], (local_heads, tok_rows))
    run_total = jnp.ones((local_heads, tok_rows), jnp.float32)
    key_count = block_part.shape[0]
    key_part = block_part[:, :HEAD_SIZE]
    value_part = block_part[:, HEAD_SIZE:].astype(jnp.float32)
    scores = (
        jnp.einsum("rhd,kd->hrk", q_rot, key_part, preferred_element_type=jnp.float32) * score_scale
    )
    visible = token_positions[:, None] >= key_pos[None, :]
    scores = jnp.where(visible[None, :, :], scores, neg_large)
    new_max = jnp.maximum(run_max, jnp.max(scores, axis=2))
    weights = jnp.exp(scores - new_max[:, :, None])
    factor = jnp.exp(run_max - new_max)
    run_total = run_total * factor + jnp.sum(weights, axis=2)
    run_sum = jnp.einsum("hrk,kd->hrd", weights, value_part, precision=lax.Precision.HIGHEST)
    attended = (
        (run_sum / run_total[:, :, None])
        .transpose(1, 0, 2)
        .reshape(tok_rows, local_heads * HEAD_SIZE)
        .astype(jnp.bfloat16)
    )
    col_width = D // exp_count
    head_part = jnp.dot(attended, out_proj, preferred_element_type=jnp.float32).astype(jnp.bfloat16)
    head_part = head_part.reshape(tok_rows, zl_count, c_count, col_width).transpose(2, 1, 0, 3)
    head_part = lax.psum_scatter(head_part, "c", scatter_dimension=0, tiled=True)[0]
    head_cols = lax.psum_scatter(head_part, "zl", scatter_dimension=0, tiled=True)[0]
    residual_cols = lax.dynamic_slice_in_dim(
        hidden_in, exp_index * col_width, col_width, 1
    ).astype(jnp.float32) + head_cols.astype(jnp.float32)
    square_part = jnp.sum(residual_cols * residual_cols, axis=1)
    square_high = square_part.astype(jnp.bfloat16)
    square_low = (square_part - square_high.astype(jnp.float32)).astype(jnp.bfloat16)
    gain_cols = lax.dynamic_slice_in_dim(norm_gain, exp_index * col_width, col_width, 0)
    normed_cols = jnp.concatenate(
        [
            (residual_cols * gain_cols[None, :]).astype(jnp.bfloat16),
            square_high[:, None],
            square_low[:, None],
        ],
        axis=1,
    )
    send_width = col_width + 2
    exp_local = gate_up.shape[0]
    n_experts = exp_local * ctx_count
    top_count = expert_ids.shape[1]
    capacity = max(2, tok_rows * top_count * 5 // (4 * n_experts))
    slot_index = route_slots(expert_ids, n_experts)
    dest_row = expert_ids * capacity + slot_index
    spread_rows = jnp.broadcast_to(
        normed_cols[:, None, :], (tok_rows, top_count, send_width)
    ).reshape(tok_rows * top_count, send_width)
    send_rows = (
        jnp.zeros((n_experts * capacity, send_width), jnp.bfloat16)
        .at[dest_row.reshape(-1)]
        .set(spread_rows)
    )
    bucket_rows = ctx_count * capacity
    unit_count = gate_up.shape[-1]
    received = lax.all_to_all(
        send_rows.reshape(ctx_count, exp_local * capacity, send_width),
        CTX,
        split_axis=0,
        concat_axis=0,
        tiled=True,
    ).reshape(bucket_rows, send_width)
    gathered = lax.all_gather(received, "zl", axis=0, tiled=False)
    gathered = lax.all_gather(gathered, "c", axis=0, tiled=False)
    row_squares = jnp.sum(
        gathered[:, :, :, col_width].astype(jnp.float32)
        + gathered[:, :, :, col_width + 1].astype(jnp.float32),
        axis=(0, 1),
    )
    row_scale = lax.rsqrt(row_squares / D + 1e-05)
    weights_flat = gate_up.reshape(zl_count, c_count, col_width, 2 * unit_count)
    gate_up_out = jnp.einsum(
        "czrk,zckf->rf",
        gathered[:, :, :, :col_width],
        weights_flat,
        preferred_element_type=jnp.float32,
    ) * row_scale[:, None]
    gate_up_out = gate_up_out.reshape(bucket_rows, 2, unit_count)
    gate_value = gate_up_out[:, 0]
    up_value = gate_up_out[:, 1]
    activated = ((up_value + 1.0) * gate_value * jax.nn.sigmoid(1.702 * gate_value)).astype(
        jnp.bfloat16
    )
    down_local = down_proj.reshape(unit_count, zl_count, c_count, col_width)
    partial_value = jnp.einsum(
        "rf,fzcd->czrd", activated, down_local, preferred_element_type=jnp.float32
    ).astype(jnp.bfloat16)
    partial_value = lax.psum_scatter(partial_value, "c", scatter_dimension=0, tiled=True)[0]
    expert_cols = lax.psum_scatter(partial_value, "zl", scatter_dimension=0, tiled=True)[0]
    returned = lax.all_to_all(
        expert_cols.reshape(ctx_count, capacity, col_width),
        CTX,
        split_axis=0,
        concat_axis=0,
        tiled=True,
    )
    picked_rows = returned.reshape(n_experts * capacity, col_width)[dest_row]
    moe_cols = jnp.sum(expert_gates[:, :, None] * picked_rows.astype(jnp.float32), axis=1)
    return (residual_cols + moe_cols).astype(jnp.bfloat16)


def solution(mesh):
    ctx_count, exp_count = mesh.devices.shape
    zh, y, x = (mesh.devices.shape[0] // 16, 4, 4)
    c_count = 2
    zl_count = exp_count // c_count
    fine = Mesh(mesh.devices.reshape(zh, y, x, zl_count, c_count), ("zh", "y", "x", "zl", "c"))
    placed = (
        P(CTX, None),
        P(CTX, EXP),
        P(CTX, None),
        P(CTX, None),
        P(EXP),
        P(EXP, None),
        P(),
        P(CTX, None),
        P(CTX, None),
        P(CTX, None, None, EXP),
        P(CTX, EXP, None),
    )
    return jax.shard_map(
        functools.partial(per_device, ctx_count=ctx_count, zl_count=zl_count, c_count=c_count),
        mesh=fine,
        in_specs=placed,
        out_specs=P(CTX, EXP),
        check_vma=False,
    )
```

```python
import functools
import math

import jax
import jax.numpy as jnp
import numpy as np
from jax import lax
from jax.sharding import Mesh, PartitionSpec as P

D = 2880
QUERY_HEADS = 32
KEY_VALUE_HEADS = 4
HEAD_SIZE = 64


yarn_base = 150000.0
yarn_factor = 32.0
yarn_initial = 4096.0
beta_fast = 32.0
beta_slow = 1.0
neg_large = -1e30


def yarn_frequencies(head_dim):
    half_dim = head_dim // 2

    def correction(rotations):
        return (
            head_dim
            * math.log(yarn_initial / (rotations * 2.0 * math.pi))
            / (2.0 * math.log(yarn_base))
        )

    lower_dim = max(math.floor(correction(beta_fast)), 0)
    upper_dim = min(math.ceil(correction(beta_slow)), head_dim - 1)
    extrap_freq = 1.0 / yarn_base ** (np.arange(0, head_dim, 2) / head_dim)
    interp_freq = extrap_freq / yarn_factor
    ramp_part = np.clip((np.arange(half_dim) - lower_dim) / (upper_dim - lower_dim), 0.0, 1.0)
    extrap_share = 1.0 - ramp_part
    return (interp_freq * (1.0 - extrap_share) + extrap_freq * extrap_share).astype(np.float32)


def rotate_with_yarn(heads_in, token_positions):
    head_dim = heads_in.shape[-1]
    freqs = jnp.asarray(yarn_frequencies(head_dim))
    angles = token_positions.astype(jnp.float32)[:, None] * freqs[None, :]
    factor = 0.1 * math.log(yarn_factor) + 1.0
    cosine = (jnp.cos(angles) * factor)[:, None, :]
    sine = (jnp.sin(angles) * factor)[:, None, :]
    first_half = heads_in[..., : head_dim // 2]
    second_half = heads_in[..., head_dim // 2 :]
    return jnp.concatenate(
        [first_half * cosine - second_half * sine, second_half * cosine + first_half * sine],
        axis=-1,
    )


def route_slots(ids_block, n_experts):
    flat_ids = ids_block.reshape(-1)
    onehot = (flat_ids[:, None] == jnp.arange(n_experts, dtype=jnp.int32)[None, :]).astype(
        jnp.int32
    )
    ranks = jnp.cumsum(onehot, axis=0) - onehot
    return jnp.sum(ranks * onehot, axis=1).reshape(ids_block.shape)


CTX = ("zh", "y", "x")
EXP = ("zl", "c")


def per_device(
    hidden_in,
    query_input,
    key_heads_input,
    value_heads_input,
    sink_logits,
    out_proj,
    norm_gain,
    expert_ids,
    expert_gates,
    gate_up,
    down_proj,
    *,
    ctx_count,
    zl_count,
    c_count,
):
    tok_rows = hidden_in.shape[0]
    exp_count = zl_count * c_count
    local_heads = query_input.shape[1] // HEAD_SIZE
    ctx_index = lax.axis_index(CTX)
    exp_index = lax.axis_index(EXP)
    col_width = D // exp_count
    token_positions = ctx_index * tok_rows + jnp.arange(tok_rows, dtype=jnp.int32)
    q_rot = rotate_with_yarn(
        query_input.astype(jnp.float32).reshape(tok_rows, local_heads, HEAD_SIZE), token_positions
    ).astype(jnp.bfloat16)
    shared_key_head = exp_index * local_heads // (QUERY_HEADS // KEY_VALUE_HEADS)
    key_block = lax.dynamic_slice_in_dim(key_heads_input, shared_key_head * HEAD_SIZE, HEAD_SIZE, 1)
    value_block = lax.dynamic_slice_in_dim(
        value_heads_input, shared_key_head * HEAD_SIZE, HEAD_SIZE, 1
    )
    key_rot = (
        rotate_with_yarn(
            key_block.astype(jnp.float32).reshape(tok_rows, 1, HEAD_SIZE), token_positions
        )
        .reshape(tok_rows, HEAD_SIZE)
        .astype(jnp.bfloat16)
    )
    key_value = jnp.concatenate([key_rot, value_block], axis=1)
    score_scale = 1.0 / math.sqrt(HEAD_SIZE)
    block_part = lax.all_gather(key_value, "zh", axis=0, tiled=False)
    block_part = lax.all_gather(block_part, "y", axis=0, tiled=False)
    block_part = lax.all_gather(block_part, "x", axis=0, tiled=False)
    zh_count = block_part.shape[2]
    y_count = block_part.shape[1]
    x_count = block_part.shape[0]
    block_of_key = (
        lax.broadcasted_iota(jnp.int32, (x_count, y_count, zh_count), 2) * (y_count * x_count)
        + lax.broadcasted_iota(jnp.int32, (x_count, y_count, zh_count), 1) * x_count
        + lax.broadcasted_iota(jnp.int32, (x_count, y_count, zh_count), 0)
    )
    key_pos = (
        block_of_key[:, :, :, None] * tok_rows + jnp.arange(tok_rows, dtype=jnp.int32)
    ).reshape(-1)
    block_part = block_part.reshape(-1, 2 * HEAD_SIZE)
    run_max = jnp.broadcast_to(sink_logits[:, None], (local_heads, tok_rows))
    run_total = jnp.ones((local_heads, tok_rows), jnp.float32)
    key_count = block_part.shape[0]
    key_part = block_part[:, :HEAD_SIZE]
    value_part = block_part[:, HEAD_SIZE:].astype(jnp.float32)
    scores = (
        jnp.einsum("rhd,kd->hrk", q_rot, key_part, preferred_element_type=jnp.float32) * score_scale
    )
    visible = token_positions[:, None] >= key_pos[None, :]
    scores = jnp.where(visible[None, :, :], scores, neg_large)
    new_max = jnp.maximum(run_max, jnp.max(scores, axis=2))
    weights = jnp.exp(scores - new_max[:, :, None])
    factor = jnp.exp(run_max - new_max)
    run_total = run_total * factor + jnp.sum(weights, axis=2)
    run_sum = jnp.einsum("hrk,kd->hrd", weights, value_part, precision=lax.Precision.HIGHEST)
    attended = (
        (run_sum / run_total[:, :, None])
        .transpose(1, 0, 2)
        .reshape(tok_rows, local_heads * HEAD_SIZE)
        .astype(jnp.bfloat16)
    )
    head_part = jnp.dot(attended, out_proj, preferred_element_type=jnp.float32).astype(jnp.bfloat16)
    head_part = head_part.reshape(tok_rows, exp_count, col_width).transpose(1, 0, 2)
    head_part = lax.all_to_all(head_part, EXP, split_axis=0, concat_axis=0, tiled=True)
    head_cols = jnp.sum(head_part.astype(jnp.float32), axis=0)
    residual_cols = lax.dynamic_slice_in_dim(
        hidden_in, exp_index * col_width, col_width, 1
    ).astype(jnp.float32) + head_cols
    square_part = jnp.sum(residual_cols * residual_cols, axis=1)
    square_high = square_part.astype(jnp.bfloat16)
    square_low = (square_part - square_high.astype(jnp.float32)).astype(jnp.bfloat16)
    gain_cols = lax.dynamic_slice_in_dim(norm_gain, exp_index * col_width, col_width, 0)
    normed_cols = jnp.concatenate(
        [
            (residual_cols * gain_cols[None, :]).astype(jnp.bfloat16),
            square_high[:, None],
            square_low[:, None],
        ],
        axis=1,
    )
    send_width = col_width + 2
    exp_local = gate_up.shape[0]
    n_experts = exp_local * ctx_count
    top_count = expert_ids.shape[1]
    capacity = max(2, tok_rows * top_count * 5 // (4 * n_experts))
    slot_index = route_slots(expert_ids, n_experts)
    dest_row = expert_ids * capacity + slot_index
    spread_rows = jnp.broadcast_to(
        normed_cols[:, None, :], (tok_rows, top_count, send_width)
    ).reshape(tok_rows * top_count, send_width)
    send_rows = (
        jnp.zeros((n_experts * capacity, send_width), jnp.bfloat16)
        .at[dest_row.reshape(-1)]
        .set(spread_rows)
    )
    bucket_rows = ctx_count * capacity
    unit_count = gate_up.shape[-1]
    received = lax.all_to_all(
        send_rows.reshape(ctx_count, exp_local * capacity, send_width),
        CTX,
        split_axis=0,
        concat_axis=0,
        tiled=True,
    ).reshape(bucket_rows, send_width)
    gathered = lax.all_gather(received, "zl", axis=0, tiled=False)
    gathered = lax.all_gather(gathered, "c", axis=0, tiled=False)
    row_squares = jnp.sum(
        gathered[:, :, :, col_width].astype(jnp.float32)
        + gathered[:, :, :, col_width + 1].astype(jnp.float32),
        axis=(0, 1),
    )
    row_scale = lax.rsqrt(row_squares / D + 1e-05)
    weights_flat = gate_up.reshape(zl_count, c_count, col_width, 2 * unit_count)
    gate_up_out = jnp.einsum(
        "czrk,zckf->rf",
        gathered[:, :, :, :col_width],
        weights_flat,
        preferred_element_type=jnp.float32,
    ) * row_scale[:, None]
    gate_up_out = gate_up_out.reshape(bucket_rows, 2, unit_count)
    gate_value = gate_up_out[:, 0]
    up_value = gate_up_out[:, 1]
    activated = ((up_value + 1.0) * gate_value * jax.nn.sigmoid(1.702 * gate_value)).astype(
        jnp.bfloat16
    )
    down_local = down_proj.reshape(unit_count, zl_count, c_count, col_width)
    partial_value = jnp.einsum(
        "rf,fzcd->czrd", activated, down_local, preferred_element_type=jnp.float32
    ).astype(jnp.bfloat16)
    partial_value = lax.psum_scatter(partial_value, "c", scatter_dimension=0, tiled=True)[0]
    expert_cols = lax.psum_scatter(partial_value, "zl", scatter_dimension=0, tiled=True)[0]
    returned = lax.all_to_all(
        expert_cols.reshape(ctx_count, capacity, col_width),
        CTX,
        split_axis=0,
        concat_axis=0,
        tiled=True,
    )
    picked_rows = returned.reshape(n_experts * capacity, col_width)[dest_row]
    moe_cols = jnp.sum(expert_gates[:, :, None] * picked_rows.astype(jnp.float32), axis=1)
    return (residual_cols + moe_cols).astype(jnp.bfloat16)


def solution(mesh):
    ctx_count, exp_count = mesh.devices.shape
    zh, y, x = (mesh.devices.shape[0] // 16, 4, 4)
    c_count = 2
    zl_count = exp_count // c_count
    fine = Mesh(mesh.devices.reshape(zh, y, x, zl_count, c_count), ("zh", "y", "x", "zl", "c"))
    placed = (
        P(CTX, None),
        P(CTX, EXP),
        P(CTX, None),
        P(CTX, None),
        P(EXP),
        P(EXP, None),
        P(),
        P(CTX, None),
        P(CTX, None),
        P(CTX, None, None, EXP),
        P(CTX, EXP, None),
    )
    return jax.shard_map(
        functools.partial(per_device, ctx_count=ctx_count, zl_count=zl_count, c_count=c_count),
        mesh=fine,
        in_specs=placed,
        out_specs=P(CTX, EXP),
        check_vma=False,
    )
```

```python
import functools
import math

import jax
import jax.numpy as jnp
import numpy as np
from jax import lax
from jax.sharding import Mesh, PartitionSpec as P

D = 2880
QUERY_HEADS = 32
KEY_VALUE_HEADS = 4
HEAD_SIZE = 64


yarn_base = 150000.0
yarn_factor = 32.0
yarn_initial = 4096.0
beta_fast = 32.0
beta_slow = 1.0
neg_large = -1e30


def yarn_frequencies(head_dim):
    half_dim = head_dim // 2

    def correction(rotations):
        return (
            head_dim
            * math.log(yarn_initial / (rotations * 2.0 * math.pi))
            / (2.0 * math.log(yarn_base))
        )

    lower_dim = max(math.floor(correction(beta_fast)), 0)
    upper_dim = min(math.ceil(correction(beta_slow)), head_dim - 1)
    extrap_freq = 1.0 / yarn_base ** (np.arange(0, head_dim, 2) / head_dim)
    interp_freq = extrap_freq / yarn_factor
    ramp_part = np.clip((np.arange(half_dim) - lower_dim) / (upper_dim - lower_dim), 0.0, 1.0)
    extrap_share = 1.0 - ramp_part
    return (interp_freq * (1.0 - extrap_share) + extrap_freq * extrap_share).astype(np.float32)


def rotate_with_yarn(heads_in, token_positions):
    head_dim = heads_in.shape[-1]
    freqs = jnp.asarray(yarn_frequencies(head_dim))
    angles = token_positions.astype(jnp.float32)[:, None] * freqs[None, :]
    factor = 0.1 * math.log(yarn_factor) + 1.0
    cosine = (jnp.cos(angles) * factor)[:, None, :]
    sine = (jnp.sin(angles) * factor)[:, None, :]
    first_half = heads_in[..., : head_dim // 2]
    second_half = heads_in[..., head_dim // 2 :]
    return jnp.concatenate(
        [first_half * cosine - second_half * sine, second_half * cosine + first_half * sine],
        axis=-1,
    )


def route_slots(ids_block, n_experts):
    flat_ids = ids_block.reshape(-1)
    onehot = (flat_ids[:, None] == jnp.arange(n_experts, dtype=jnp.int32)[None, :]).astype(
        jnp.int32
    )
    ranks = jnp.cumsum(onehot, axis=0) - onehot
    return jnp.sum(ranks * onehot, axis=1).reshape(ids_block.shape)


CTX = ("zh", "y", "x")
ZL = ("zlh", "zll")
EXP = ("zlh", "zll", "c")


def per_device(
    hidden_in,
    query_input,
    key_heads_input,
    value_heads_input,
    sink_logits,
    out_proj,
    norm_gain,
    expert_ids,
    expert_gates,
    gate_up,
    down_proj,
    *,
    ctx_count,
    zl_count,
    c_count,
):
    tok_rows = hidden_in.shape[0]
    exp_count = zl_count * c_count
    local_heads = query_input.shape[1] // HEAD_SIZE
    ctx_index = lax.axis_index(CTX)
    exp_index = lax.axis_index(EXP)
    col_width = D // exp_count
    token_positions = ctx_index * tok_rows + jnp.arange(tok_rows, dtype=jnp.int32)
    q_rot = rotate_with_yarn(
        query_input.astype(jnp.float32).reshape(tok_rows, local_heads, HEAD_SIZE), token_positions
    ).astype(jnp.bfloat16)
    shared_key_head = exp_index * local_heads // (QUERY_HEADS // KEY_VALUE_HEADS)
    key_block = lax.dynamic_slice_in_dim(key_heads_input, shared_key_head * HEAD_SIZE, HEAD_SIZE, 1)
    value_block = lax.dynamic_slice_in_dim(
        value_heads_input, shared_key_head * HEAD_SIZE, HEAD_SIZE, 1
    )
    key_rot = (
        rotate_with_yarn(
            key_block.astype(jnp.float32).reshape(tok_rows, 1, HEAD_SIZE), token_positions
        )
        .reshape(tok_rows, HEAD_SIZE)
        .astype(jnp.bfloat16)
    )
    key_value = jnp.concatenate([key_rot, value_block], axis=1)
    score_scale = 1.0 / math.sqrt(HEAD_SIZE)
    block_part = lax.all_gather(key_value, "zh", axis=0, tiled=False)
    block_part = lax.all_gather(block_part, "y", axis=0, tiled=False)
    block_part = lax.all_gather(block_part, "x", axis=0, tiled=False)
    zh_count = block_part.shape[2]
    y_count = block_part.shape[1]
    x_count = block_part.shape[0]
    block_of_key = (
        lax.broadcasted_iota(jnp.int32, (x_count, y_count, zh_count), 2) * (y_count * x_count)
        + lax.broadcasted_iota(jnp.int32, (x_count, y_count, zh_count), 1) * x_count
        + lax.broadcasted_iota(jnp.int32, (x_count, y_count, zh_count), 0)
    )
    key_pos = (
        block_of_key[:, :, :, None] * tok_rows + jnp.arange(tok_rows, dtype=jnp.int32)
    ).reshape(-1)
    block_part = block_part.reshape(-1, 2 * HEAD_SIZE)
    run_max = jnp.broadcast_to(sink_logits[:, None], (local_heads, tok_rows))
    run_total = jnp.ones((local_heads, tok_rows), jnp.float32)
    key_count = block_part.shape[0]
    key_part = block_part[:, :HEAD_SIZE]
    value_part = block_part[:, HEAD_SIZE:].astype(jnp.float32)
    scores = (
        jnp.einsum("rhd,kd->hrk", q_rot, key_part, preferred_element_type=jnp.float32) * score_scale
    )
    visible = token_positions[:, None] >= key_pos[None, :]
    scores = jnp.where(visible[None, :, :], scores, neg_large)
    new_max = jnp.maximum(run_max, jnp.max(scores, axis=2))
    weights = jnp.exp(scores - new_max[:, :, None])
    factor = jnp.exp(run_max - new_max)
    run_total = run_total * factor + jnp.sum(weights, axis=2)
    run_sum = jnp.einsum("hrk,kd->hrd", weights, value_part, precision=lax.Precision.HIGHEST)
    attended = (
        (run_sum / run_total[:, :, None])
        .transpose(1, 0, 2)
        .reshape(tok_rows, local_heads * HEAD_SIZE)
        .astype(jnp.bfloat16)
    )
    head_part = jnp.dot(attended, out_proj, preferred_element_type=jnp.float32).astype(jnp.bfloat16)
    head_part = head_part.reshape(tok_rows, exp_count, col_width).transpose(1, 0, 2)
    head_part = lax.all_to_all(head_part, EXP, split_axis=0, concat_axis=0, tiled=True)
    head_cols = jnp.sum(head_part.astype(jnp.float32), axis=0)
    residual_cols = lax.dynamic_slice_in_dim(
        hidden_in, exp_index * col_width, col_width, 1
    ).astype(jnp.float32) + head_cols
    square_part = jnp.sum(residual_cols * residual_cols, axis=1)
    square_high = square_part.astype(jnp.bfloat16)
    square_low = (square_part - square_high.astype(jnp.float32)).astype(jnp.bfloat16)
    gain_cols = lax.dynamic_slice_in_dim(norm_gain, exp_index * col_width, col_width, 0)
    normed_cols = jnp.concatenate(
        [
            (residual_cols * gain_cols[None, :]).astype(jnp.bfloat16),
            square_high[:, None],
            square_low[:, None],
        ],
        axis=1,
    )
    send_width = col_width + 2
    exp_local = gate_up.shape[0]
    n_experts = exp_local * ctx_count
    top_count = expert_ids.shape[1]
    capacity = max(2, tok_rows * top_count * 5 // (4 * n_experts))
    slot_index = route_slots(expert_ids, n_experts)
    dest_row = expert_ids * capacity + slot_index
    spread_rows = jnp.broadcast_to(
        normed_cols[:, None, :], (tok_rows, top_count, send_width)
    ).reshape(tok_rows * top_count, send_width)
    send_rows = (
        jnp.zeros((n_experts * capacity, send_width), jnp.bfloat16)
        .at[dest_row.reshape(-1)]
        .set(spread_rows)
    )
    bucket_rows = ctx_count * capacity
    unit_count = gate_up.shape[-1]
    received = lax.all_to_all(
        send_rows.reshape(ctx_count, exp_local * capacity, send_width),
        CTX,
        split_axis=0,
        concat_axis=0,
        tiled=True,
    ).reshape(bucket_rows, send_width)
    gathered = lax.all_gather(received, ZL, axis=0, tiled=False)
    gathered = lax.all_gather(gathered, "c", axis=0, tiled=False)
    row_squares = jnp.sum(
        gathered[:, :, :, col_width].astype(jnp.float32)
        + gathered[:, :, :, col_width + 1].astype(jnp.float32),
        axis=(0, 1),
    )
    row_scale = lax.rsqrt(row_squares / D + 1e-05)
    weights_flat = gate_up.reshape(zl_count, c_count, col_width, 2 * unit_count)
    gate_up_out = jnp.einsum(
        "czrk,zckf->rf",
        gathered[:, :, :, :col_width],
        weights_flat,
        preferred_element_type=jnp.float32,
    ) * row_scale[:, None]
    gate_up_out = gate_up_out.reshape(bucket_rows, 2, unit_count)
    gate_value = gate_up_out[:, 0]
    up_value = gate_up_out[:, 1]
    activated = ((up_value + 1.0) * gate_value * jax.nn.sigmoid(1.702 * gate_value)).astype(
        jnp.bfloat16
    )
    zlh_count = zl_count // 2
    down_local = down_proj.reshape(unit_count, zlh_count, 2, c_count, col_width)
    partial_value = jnp.einsum(
        "rf,fhlcd->chlrd", activated, down_local, preferred_element_type=jnp.float32
    ).astype(jnp.bfloat16)
    partial_value = lax.all_to_all(partial_value, "c", 0, 0, tiled=True)
    partial_value = jnp.sum(partial_value.astype(jnp.float32), axis=0).astype(jnp.bfloat16)
    partial_value = lax.all_to_all(partial_value.transpose(1, 0, 2, 3), "zll", 0, 0, tiled=True)
    partial_value = jnp.sum(partial_value.astype(jnp.float32), axis=0).astype(jnp.bfloat16)
    partial_value = lax.all_to_all(partial_value, "zlh", 0, 0, tiled=True)
    expert_cols = jnp.sum(partial_value.astype(jnp.float32), axis=0).astype(jnp.bfloat16)
    returned = lax.all_to_all(
        expert_cols.reshape(ctx_count, capacity, col_width),
        CTX,
        split_axis=0,
        concat_axis=0,
        tiled=True,
    )
    picked_rows = returned.reshape(n_experts * capacity, col_width)[dest_row]
    moe_cols = jnp.sum(expert_gates[:, :, None] * picked_rows.astype(jnp.float32), axis=1)
    return (residual_cols + moe_cols).astype(jnp.bfloat16)


def solution(mesh):
    ctx_count, exp_count = mesh.devices.shape
    zh, y, x = (mesh.devices.shape[0] // 16, 4, 4)
    c_count = 2
    zl_count = exp_count // c_count
    fine = Mesh(
        mesh.devices.reshape(zh, y, x, zl_count // 2, 2, c_count), ("zh", "y", "x", "zlh", "zll", "c")
    )
    placed = (
        P(CTX, None),
        P(CTX, EXP),
        P(CTX, None),
        P(CTX, None),
        P(EXP),
        P(EXP, None),
        P(),
        P(CTX, None),
        P(CTX, None),
        P(CTX, None, None, EXP),
        P(CTX, EXP, None),
    )
    return jax.shard_map(
        functools.partial(per_device, ctx_count=ctx_count, zl_count=zl_count, c_count=c_count),
        mesh=fine,
        in_specs=placed,
        out_specs=P(CTX, EXP),
        check_vma=False,
    )
```

```python
import functools
import math

import jax
import jax.numpy as jnp
import numpy as np
from jax import lax
from jax.sharding import Mesh, PartitionSpec as P

D = 2880
QUERY_HEADS = 32
KEY_VALUE_HEADS = 4
HEAD_SIZE = 64


yarn_base = 150000.0
yarn_factor = 32.0
yarn_initial = 4096.0
beta_fast = 32.0
beta_slow = 1.0
neg_large = -1e30


def yarn_frequencies(head_dim):
    half_dim = head_dim // 2

    def correction(rotations):
        return (
            head_dim
            * math.log(yarn_initial / (rotations * 2.0 * math.pi))
            / (2.0 * math.log(yarn_base))
        )

    lower_dim = max(math.floor(correction(beta_fast)), 0)
    upper_dim = min(math.ceil(correction(beta_slow)), head_dim - 1)
    extrap_freq = 1.0 / yarn_base ** (np.arange(0, head_dim, 2) / head_dim)
    interp_freq = extrap_freq / yarn_factor
    ramp_part = np.clip((np.arange(half_dim) - lower_dim) / (upper_dim - lower_dim), 0.0, 1.0)
    extrap_share = 1.0 - ramp_part
    return (interp_freq * (1.0 - extrap_share) + extrap_freq * extrap_share).astype(np.float32)


def rotate_with_yarn(heads_in, token_positions):
    head_dim = heads_in.shape[-1]
    freqs = jnp.asarray(yarn_frequencies(head_dim))
    angles = token_positions.astype(jnp.float32)[:, None] * freqs[None, :]
    factor = 0.1 * math.log(yarn_factor) + 1.0
    cosine = (jnp.cos(angles) * factor)[:, None, :]
    sine = (jnp.sin(angles) * factor)[:, None, :]
    first_half = heads_in[..., : head_dim // 2]
    second_half = heads_in[..., head_dim // 2 :]
    return jnp.concatenate(
        [first_half * cosine - second_half * sine, second_half * cosine + first_half * sine],
        axis=-1,
    )


def route_slots(ids_block, n_experts):
    flat_ids = ids_block.reshape(-1)
    onehot = (flat_ids[:, None] == jnp.arange(n_experts, dtype=jnp.int32)[None, :]).astype(
        jnp.int32
    )
    ranks = jnp.cumsum(onehot, axis=0) - onehot
    return jnp.sum(ranks * onehot, axis=1).reshape(ids_block.shape)


CTX = ("zh", "y", "x")
ZL = ("zlh", "zll")
EXP = ("zlh", "zll", "c")


def per_device(
    hidden_in,
    query_input,
    key_heads_input,
    value_heads_input,
    sink_logits,
    out_proj,
    norm_gain,
    expert_ids,
    expert_gates,
    gate_up,
    down_proj,
    *,
    ctx_count,
    zl_count,
    c_count,
):
    tok_rows = hidden_in.shape[0]
    exp_count = zl_count * c_count
    local_heads = query_input.shape[1] // HEAD_SIZE
    ctx_index = lax.axis_index(CTX)
    exp_index = lax.axis_index(EXP)
    col_width = D // exp_count
    token_positions = ctx_index * tok_rows + jnp.arange(tok_rows, dtype=jnp.int32)
    q_rot = rotate_with_yarn(
        query_input.astype(jnp.float32).reshape(tok_rows, local_heads, HEAD_SIZE), token_positions
    ).astype(jnp.bfloat16)
    shared_key_head = exp_index * local_heads // (QUERY_HEADS // KEY_VALUE_HEADS)
    key_block = lax.dynamic_slice_in_dim(key_heads_input, shared_key_head * HEAD_SIZE, HEAD_SIZE, 1)
    value_block = lax.dynamic_slice_in_dim(
        value_heads_input, shared_key_head * HEAD_SIZE, HEAD_SIZE, 1
    )
    key_rot = (
        rotate_with_yarn(
            key_block.astype(jnp.float32).reshape(tok_rows, 1, HEAD_SIZE), token_positions
        )
        .reshape(tok_rows, HEAD_SIZE)
        .astype(jnp.bfloat16)
    )
    key_value = jnp.concatenate([key_rot, value_block], axis=1)
    score_scale = 1.0 / math.sqrt(HEAD_SIZE)
    block_part = lax.all_gather(key_value, "zh", axis=0, tiled=False)
    block_part = lax.all_gather(block_part, ("y", "x"), axis=0, tiled=False)
    zh_count = block_part.shape[1]
    plane_count = block_part.shape[0]
    block_of_key = (
        lax.broadcasted_iota(jnp.int32, (plane_count, zh_count), 1) * plane_count
        + lax.broadcasted_iota(jnp.int32, (plane_count, zh_count), 0)
    )
    key_pos = (
        block_of_key[:, :, None] * tok_rows + jnp.arange(tok_rows, dtype=jnp.int32)
    ).reshape(-1)
    block_part = block_part.reshape(-1, 2 * HEAD_SIZE)
    run_max = jnp.broadcast_to(sink_logits[:, None], (local_heads, tok_rows))
    run_total = jnp.ones((local_heads, tok_rows), jnp.float32)
    key_count = block_part.shape[0]
    key_part = block_part[:, :HEAD_SIZE]
    value_part = block_part[:, HEAD_SIZE:].astype(jnp.float32)
    scores = (
        jnp.einsum("rhd,kd->hrk", q_rot, key_part, preferred_element_type=jnp.float32) * score_scale
    )
    visible = token_positions[:, None] >= key_pos[None, :]
    scores = jnp.where(visible[None, :, :], scores, neg_large)
    new_max = jnp.maximum(run_max, jnp.max(scores, axis=2))
    weights = jnp.exp(scores - new_max[:, :, None])
    factor = jnp.exp(run_max - new_max)
    run_total = run_total * factor + jnp.sum(weights, axis=2)
    run_sum = jnp.einsum("hrk,kd->hrd", weights, value_part, precision=lax.Precision.HIGHEST)
    attended = (
        (run_sum / run_total[:, :, None])
        .transpose(1, 0, 2)
        .reshape(tok_rows, local_heads * HEAD_SIZE)
        .astype(jnp.bfloat16)
    )
    head_part = jnp.dot(attended, out_proj, preferred_element_type=jnp.float32).astype(jnp.bfloat16)
    head_part = head_part.reshape(tok_rows, zl_count, c_count, col_width).transpose(2, 1, 0, 3)
    head_part = lax.all_to_all(head_part, "c", split_axis=0, concat_axis=0, tiled=True)
    head_part = jnp.sum(head_part.astype(jnp.float32), axis=0).astype(jnp.bfloat16)
    head_part = lax.all_to_all(head_part, ZL, split_axis=0, concat_axis=0, tiled=True)
    head_cols = jnp.sum(head_part.astype(jnp.float32), axis=0)
    residual_cols = lax.dynamic_slice_in_dim(
        hidden_in, exp_index * col_width, col_width, 1
    ).astype(jnp.float32) + head_cols
    square_part = jnp.sum(residual_cols * residual_cols, axis=1)
    square_high = square_part.astype(jnp.bfloat16)
    square_low = (square_part - square_high.astype(jnp.float32)).astype(jnp.bfloat16)
    gain_cols = lax.dynamic_slice_in_dim(norm_gain, exp_index * col_width, col_width, 0)
    normed_cols = jnp.concatenate(
        [
            (residual_cols * gain_cols[None, :]).astype(jnp.bfloat16),
            square_high[:, None],
            square_low[:, None],
        ],
        axis=1,
    )
    send_width = col_width + 2
    exp_local = gate_up.shape[0]
    n_experts = exp_local * ctx_count
    top_count = expert_ids.shape[1]
    capacity = max(2, tok_rows * top_count * 5 // (4 * n_experts))
    slot_index = route_slots(expert_ids, n_experts)
    dest_row = expert_ids * capacity + slot_index
    spread_rows = jnp.broadcast_to(
        normed_cols[:, None, :], (tok_rows, top_count, send_width)
    ).reshape(tok_rows * top_count, send_width)
    send_rows = (
        jnp.zeros((n_experts * capacity, send_width), jnp.bfloat16)
        .at[dest_row.reshape(-1)]
        .set(spread_rows)
    )
    bucket_rows = ctx_count * capacity
    unit_count = gate_up.shape[-1]
    received = lax.all_to_all(
        send_rows.reshape(ctx_count, exp_local * capacity, send_width),
        CTX,
        split_axis=0,
        concat_axis=0,
        tiled=True,
    ).reshape(bucket_rows, send_width)
    gathered = lax.all_gather(received, ZL, axis=0, tiled=False)
    gathered = lax.all_gather(gathered, "c", axis=0, tiled=False)
    row_squares = jnp.sum(
        gathered[:, :, :, col_width].astype(jnp.float32)
        + gathered[:, :, :, col_width + 1].astype(jnp.float32),
        axis=(0, 1),
    )
    row_scale = lax.rsqrt(row_squares / D + 1e-05)
    weights_flat = gate_up.reshape(zl_count, c_count, col_width, 2 * unit_count)
    gate_up_out = jnp.einsum(
        "czrk,zckf->rf",
        gathered[:, :, :, :col_width],
        weights_flat,
        preferred_element_type=jnp.float32,
    ) * row_scale[:, None]
    gate_up_out = gate_up_out.reshape(bucket_rows, 2, unit_count)
    gate_value = gate_up_out[:, 0]
    up_value = gate_up_out[:, 1]
    activated = ((up_value + 1.0) * gate_value * jax.nn.sigmoid(1.702 * gate_value)).astype(
        jnp.bfloat16
    )
    zlh_count = zl_count // 2
    down_local = down_proj.reshape(unit_count, zlh_count, 2, c_count, col_width)
    partial_value = jnp.einsum(
        "rf,fhlcd->chlrd", activated, down_local, preferred_element_type=jnp.float32
    ).astype(jnp.bfloat16)
    partial_value = lax.all_to_all(partial_value, "c", 0, 0, tiled=True)
    partial_value = jnp.sum(partial_value.astype(jnp.float32), axis=0).astype(jnp.bfloat16)
    partial_value = lax.all_to_all(partial_value.transpose(1, 0, 2, 3), "zll", 0, 0, tiled=True)
    partial_value = jnp.sum(partial_value.astype(jnp.float32), axis=0).astype(jnp.bfloat16)
    partial_value = lax.all_to_all(partial_value, "zlh", 0, 0, tiled=True)
    expert_cols = jnp.sum(partial_value.astype(jnp.float32), axis=0).astype(jnp.bfloat16)
    returned = lax.all_to_all(
        expert_cols.reshape(ctx_count, capacity, col_width),
        CTX,
        split_axis=0,
        concat_axis=0,
        tiled=True,
    )
    picked_rows = returned.reshape(n_experts * capacity, col_width)[dest_row]
    moe_cols = jnp.sum(expert_gates[:, :, None] * picked_rows.astype(jnp.float32), axis=1)
    return (residual_cols + moe_cols).astype(jnp.bfloat16)


def solution(mesh):
    ctx_count, exp_count = mesh.devices.shape
    zh, y, x = (mesh.devices.shape[0] // 16, 4, 4)
    c_count = 2
    zl_count = exp_count // c_count
    fine = Mesh(
        mesh.devices.reshape(zh, y, x, zl_count // 2, 2, c_count), ("zh", "y", "x", "zlh", "zll", "c")
    )
    placed = (
        P(CTX, None),
        P(CTX, EXP),
        P(CTX, None),
        P(CTX, None),
        P(EXP),
        P(EXP, None),
        P(),
        P(CTX, None),
        P(CTX, None),
        P(CTX, None, None, EXP),
        P(CTX, EXP, None),
    )
    return jax.shard_map(
        functools.partial(per_device, ctx_count=ctx_count, zl_count=zl_count, c_count=c_count),
        mesh=fine,
        in_specs=placed,
        out_specs=P(CTX, EXP),
        check_vma=False,
    )
```

```python
import functools
import math

import jax
import jax.numpy as jnp
import numpy as np
from jax import lax
from jax.sharding import Mesh, PartitionSpec as P

D = 2880
QUERY_HEADS = 32
KEY_VALUE_HEADS = 4
HEAD_SIZE = 64


yarn_base = 150000.0
yarn_factor = 32.0
yarn_initial = 4096.0
beta_fast = 32.0
beta_slow = 1.0
neg_large = -1e30


def yarn_frequencies(head_dim):
    half_dim = head_dim // 2

    def correction(rotations):
        return (
            head_dim
            * math.log(yarn_initial / (rotations * 2.0 * math.pi))
            / (2.0 * math.log(yarn_base))
        )

    lower_dim = max(math.floor(correction(beta_fast)), 0)
    upper_dim = min(math.ceil(correction(beta_slow)), head_dim - 1)
    extrap_freq = 1.0 / yarn_base ** (np.arange(0, head_dim, 2) / head_dim)
    interp_freq = extrap_freq / yarn_factor
    ramp_part = np.clip((np.arange(half_dim) - lower_dim) / (upper_dim - lower_dim), 0.0, 1.0)
    extrap_share = 1.0 - ramp_part
    return (interp_freq * (1.0 - extrap_share) + extrap_freq * extrap_share).astype(np.float32)


def rotate_with_yarn(heads_in, token_positions):
    head_dim = heads_in.shape[-1]
    freqs = jnp.asarray(yarn_frequencies(head_dim))
    angles = token_positions.astype(jnp.float32)[:, None] * freqs[None, :]
    factor = 0.1 * math.log(yarn_factor) + 1.0
    cosine = (jnp.cos(angles) * factor)[:, None, :]
    sine = (jnp.sin(angles) * factor)[:, None, :]
    first_half = heads_in[..., : head_dim // 2]
    second_half = heads_in[..., head_dim // 2 :]
    return jnp.concatenate(
        [first_half * cosine - second_half * sine, second_half * cosine + first_half * sine],
        axis=-1,
    )


def route_slots(ids_block, n_experts):
    flat_ids = ids_block.reshape(-1)
    onehot = (flat_ids[:, None] == jnp.arange(n_experts, dtype=jnp.int32)[None, :]).astype(
        jnp.int32
    )
    ranks = jnp.cumsum(onehot, axis=0) - onehot
    return jnp.sum(ranks * onehot, axis=1).reshape(ids_block.shape)


CTX = ("zh", "y", "x")
ZL = ("zlh", "zll")
EXP = ("zlh", "zll", "c")


def per_device(
    hidden_in,
    query_input,
    key_heads_input,
    value_heads_input,
    sink_logits,
    out_proj,
    norm_gain,
    expert_ids,
    expert_gates,
    gate_up,
    down_proj,
    *,
    ctx_count,
    zl_count,
    c_count,
):
    tok_rows = hidden_in.shape[0]
    exp_count = zl_count * c_count
    local_heads = query_input.shape[1] // HEAD_SIZE
    ctx_index = lax.axis_index(CTX)
    exp_index = lax.axis_index(EXP)
    col_width = D // exp_count
    token_positions = ctx_index * tok_rows + jnp.arange(tok_rows, dtype=jnp.int32)
    q_rot = rotate_with_yarn(
        query_input.astype(jnp.float32).reshape(tok_rows, local_heads, HEAD_SIZE), token_positions
    ).astype(jnp.bfloat16)
    shared_key_head = exp_index * local_heads // (QUERY_HEADS // KEY_VALUE_HEADS)
    key_block = lax.dynamic_slice_in_dim(key_heads_input, shared_key_head * HEAD_SIZE, HEAD_SIZE, 1)
    value_block = lax.dynamic_slice_in_dim(
        value_heads_input, shared_key_head * HEAD_SIZE, HEAD_SIZE, 1
    )
    key_rot = (
        rotate_with_yarn(
            key_block.astype(jnp.float32).reshape(tok_rows, 1, HEAD_SIZE), token_positions
        )
        .reshape(tok_rows, HEAD_SIZE)
        .astype(jnp.bfloat16)
    )
    key_value = jnp.concatenate([key_rot, value_block], axis=1)
    score_scale = 1.0 / math.sqrt(HEAD_SIZE)
    block_part = lax.all_gather(key_value, "zh", axis=0, tiled=False)
    block_part = lax.all_gather(block_part, "y", axis=0, tiled=False)
    block_part = lax.all_gather(block_part, "x", axis=0, tiled=False)
    zh_count = block_part.shape[2]
    y_count = block_part.shape[1]
    x_count = block_part.shape[0]
    block_of_key = (
        lax.broadcasted_iota(jnp.int32, (x_count, y_count, zh_count), 2) * (y_count * x_count)
        + lax.broadcasted_iota(jnp.int32, (x_count, y_count, zh_count), 1) * x_count
        + lax.broadcasted_iota(jnp.int32, (x_count, y_count, zh_count), 0)
    )
    key_pos = (
        block_of_key[:, :, :, None] * tok_rows + jnp.arange(tok_rows, dtype=jnp.int32)
    ).reshape(-1)
    block_part = block_part.reshape(-1, 2 * HEAD_SIZE)
    run_max = jnp.broadcast_to(sink_logits[:, None], (local_heads, tok_rows))
    run_total = jnp.ones((local_heads, tok_rows), jnp.float32)
    key_count = block_part.shape[0]
    key_part = block_part[:, :HEAD_SIZE]
    value_part = block_part[:, HEAD_SIZE:].astype(jnp.float32)
    scores = (
        jnp.einsum("rhd,kd->hrk", q_rot, key_part, preferred_element_type=jnp.float32) * score_scale
    )
    visible = token_positions[:, None] >= key_pos[None, :]
    scores = jnp.where(visible[None, :, :], scores, neg_large)
    new_max = jnp.maximum(run_max, jnp.max(scores, axis=2))
    weights = jnp.exp(scores - new_max[:, :, None])
    factor = jnp.exp(run_max - new_max)
    run_total = run_total * factor + jnp.sum(weights, axis=2)
    run_sum = jnp.einsum("hrk,kd->hrd", weights, value_part, precision=lax.Precision.HIGHEST)
    attended = (
        (run_sum / run_total[:, :, None])
        .transpose(1, 0, 2)
        .reshape(tok_rows, local_heads * HEAD_SIZE)
        .astype(jnp.bfloat16)
    )
    head_part = jnp.dot(attended, out_proj, preferred_element_type=jnp.float32).astype(jnp.bfloat16)
    head_part = head_part.reshape(tok_rows, zl_count, c_count, col_width).transpose(2, 1, 0, 3)
    head_part = lax.all_to_all(head_part, "c", split_axis=0, concat_axis=0, tiled=True)
    head_part = jnp.sum(head_part.astype(jnp.float32), axis=0).astype(jnp.bfloat16)
    head_part = lax.all_to_all(head_part, ZL, split_axis=0, concat_axis=0, tiled=True)
    head_cols = jnp.sum(head_part.astype(jnp.float32), axis=0)
    residual_cols = lax.dynamic_slice_in_dim(
        hidden_in, exp_index * col_width, col_width, 1
    ).astype(jnp.float32) + head_cols
    square_part = jnp.sum(residual_cols * residual_cols, axis=1)
    square_high = square_part.astype(jnp.bfloat16)
    square_low = (square_part - square_high.astype(jnp.float32)).astype(jnp.bfloat16)
    gain_cols = lax.dynamic_slice_in_dim(norm_gain, exp_index * col_width, col_width, 0)
    normed_cols = jnp.concatenate(
        [
            (residual_cols * gain_cols[None, :]).astype(jnp.bfloat16),
            square_high[:, None],
            square_low[:, None],
        ],
        axis=1,
    )
    send_width = col_width + 2
    exp_local = gate_up.shape[0]
    n_experts = exp_local * ctx_count
    top_count = expert_ids.shape[1]
    capacity = max(2, tok_rows * top_count * 5 // (4 * n_experts))
    slot_index = route_slots(expert_ids, n_experts)
    dest_row = expert_ids * capacity + slot_index
    spread_rows = jnp.broadcast_to(
        normed_cols[:, None, :], (tok_rows, top_count, send_width)
    ).reshape(tok_rows * top_count, send_width)
    send_rows = (
        jnp.zeros((n_experts * capacity, send_width), jnp.bfloat16)
        .at[dest_row.reshape(-1)]
        .set(spread_rows)
    )
    bucket_rows = ctx_count * capacity
    unit_count = gate_up.shape[-1]
    received = lax.all_to_all(
        send_rows.reshape(ctx_count, exp_local * capacity, send_width),
        CTX,
        split_axis=0,
        concat_axis=0,
        tiled=True,
    ).reshape(bucket_rows, send_width)
    gathered = lax.all_gather(received, ZL, axis=0, tiled=False)
    gathered = lax.all_gather(gathered, "c", axis=0, tiled=False)
    row_squares = jnp.sum(
        gathered[:, :, :, col_width].astype(jnp.float32)
        + gathered[:, :, :, col_width + 1].astype(jnp.float32),
        axis=(0, 1),
    )
    row_scale = lax.rsqrt(row_squares / D + 1e-05)
    weights_flat = gate_up.reshape(zl_count, c_count, col_width, 2 * unit_count)
    gate_up_out = jnp.einsum(
        "czrk,zckf->rf",
        gathered[:, :, :, :col_width],
        weights_flat,
        preferred_element_type=jnp.float32,
    ) * row_scale[:, None]
    gate_up_out = gate_up_out.reshape(bucket_rows, 2, unit_count)
    gate_value = gate_up_out[:, 0]
    up_value = gate_up_out[:, 1]
    activated = ((up_value + 1.0) * gate_value * jax.nn.sigmoid(1.702 * gate_value)).astype(
        jnp.bfloat16
    )
    zlh_count = zl_count // 2
    down_local = down_proj.reshape(unit_count, zlh_count, 2, c_count, col_width)
    partial_value = jnp.einsum(
        "rf,fhlcd->chlrd", activated, down_local, preferred_element_type=jnp.float32
    ).astype(jnp.bfloat16)
    partial_value = lax.all_to_all(partial_value, "c", 0, 0, tiled=True)
    partial_value = jnp.sum(partial_value.astype(jnp.float32), axis=0).astype(jnp.bfloat16)
    partial_value = lax.all_to_all(partial_value.transpose(1, 0, 2, 3), "zll", 0, 0, tiled=True)
    partial_value = jnp.sum(partial_value.astype(jnp.float32), axis=0).astype(jnp.bfloat16)
    partial_value = lax.all_to_all(partial_value, "zlh", 0, 0, tiled=True)
    expert_cols = jnp.sum(partial_value.astype(jnp.float32), axis=0).astype(jnp.bfloat16)
    returned = lax.all_to_all(
        expert_cols.reshape(ctx_count, capacity, col_width),
        CTX,
        split_axis=0,
        concat_axis=0,
        tiled=True,
    )
    picked_rows = returned.reshape(n_experts * capacity, col_width)[dest_row]
    moe_cols = jnp.sum(expert_gates[:, :, None] * picked_rows.astype(jnp.float32), axis=1)
    return (residual_cols + moe_cols).astype(jnp.bfloat16)


def solution(mesh):
    ctx_count, exp_count = mesh.devices.shape
    zh, y, x = (mesh.devices.shape[0] // 16, 4, 4)
    c_count = 2
    zl_count = exp_count // c_count
    fine = Mesh(
        mesh.devices.reshape(zh, y, x, zl_count // 2, 2, c_count), ("zh", "y", "x", "zlh", "zll", "c")
    )
    placed = (
        P(CTX, None),
        P(CTX, EXP),
        P(CTX, None),
        P(CTX, None),
        P(EXP),
        P(EXP, None),
        P(),
        P(CTX, None),
        P(CTX, None),
        P(CTX, None, None, EXP),
        P(CTX, EXP, None),
    )
    return jax.shard_map(
        functools.partial(per_device, ctx_count=ctx_count, zl_count=zl_count, c_count=c_count),
        mesh=fine,
        in_specs=placed,
        out_specs=P(CTX, EXP),
        check_vma=False,
    )
```

```python
import functools
import math

import jax
import jax.numpy as jnp
import numpy as np
from jax import lax
from jax.sharding import Mesh, PartitionSpec as P

D = 2880
QUERY_HEADS = 32
KEY_VALUE_HEADS = 4
HEAD_SIZE = 64


yarn_base = 150000.0
yarn_factor = 32.0
yarn_initial = 4096.0
beta_fast = 32.0
beta_slow = 1.0
neg_large = -1e30


def yarn_frequencies(head_dim):
    half_dim = head_dim // 2

    def correction(rotations):
        return (
            head_dim
            * math.log(yarn_initial / (rotations * 2.0 * math.pi))
            / (2.0 * math.log(yarn_base))
        )

    lower_dim = max(math.floor(correction(beta_fast)), 0)
    upper_dim = min(math.ceil(correction(beta_slow)), head_dim - 1)
    extrap_freq = 1.0 / yarn_base ** (np.arange(0, head_dim, 2) / head_dim)
    interp_freq = extrap_freq / yarn_factor
    ramp_part = np.clip((np.arange(half_dim) - lower_dim) / (upper_dim - lower_dim), 0.0, 1.0)
    extrap_share = 1.0 - ramp_part
    return (interp_freq * (1.0 - extrap_share) + extrap_freq * extrap_share).astype(np.float32)


def rotate_with_yarn(heads_in, token_positions):
    head_dim = heads_in.shape[-1]
    freqs = jnp.asarray(yarn_frequencies(head_dim))
    angles = token_positions.astype(jnp.float32)[:, None] * freqs[None, :]
    factor = 0.1 * math.log(yarn_factor) + 1.0
    cosine = (jnp.cos(angles) * factor)[:, None, :]
    sine = (jnp.sin(angles) * factor)[:, None, :]
    first_half = heads_in[..., : head_dim // 2]
    second_half = heads_in[..., head_dim // 2 :]
    return jnp.concatenate(
        [first_half * cosine - second_half * sine, second_half * cosine + first_half * sine],
        axis=-1,
    )


def route_slots(ids_block, n_experts):
    flat_ids = ids_block.reshape(-1)
    onehot = (flat_ids[:, None] == jnp.arange(n_experts, dtype=jnp.int32)[None, :]).astype(
        jnp.int32
    )
    ranks = jnp.cumsum(onehot, axis=0) - onehot
    return jnp.sum(ranks * onehot, axis=1).reshape(ids_block.shape)


CTX = ("zh", "y", "x")
ZL = ("zb2", "zb1", "zb0")
EXP = ("zb2", "zb1", "zb0", "c")


def per_device(
    hidden_in,
    query_input,
    key_heads_input,
    value_heads_input,
    sink_logits,
    out_proj,
    norm_gain,
    expert_ids,
    expert_gates,
    gate_up,
    down_proj,
    *,
    ctx_count,
    zl_count,
    c_count,
):
    tok_rows = hidden_in.shape[0]
    exp_count = zl_count * c_count
    local_heads = query_input.shape[1] // HEAD_SIZE
    ctx_index = lax.axis_index(CTX)
    exp_index = lax.axis_index(EXP)
    col_width = D // exp_count
    token_positions = ctx_index * tok_rows + jnp.arange(tok_rows, dtype=jnp.int32)
    q_rot = rotate_with_yarn(
        query_input.astype(jnp.float32).reshape(tok_rows, local_heads, HEAD_SIZE), token_positions
    ).astype(jnp.bfloat16)
    shared_key_head = exp_index * local_heads // (QUERY_HEADS // KEY_VALUE_HEADS)
    key_block = lax.dynamic_slice_in_dim(key_heads_input, shared_key_head * HEAD_SIZE, HEAD_SIZE, 1)
    value_block = lax.dynamic_slice_in_dim(
        value_heads_input, shared_key_head * HEAD_SIZE, HEAD_SIZE, 1
    )
    key_rot = (
        rotate_with_yarn(
            key_block.astype(jnp.float32).reshape(tok_rows, 1, HEAD_SIZE), token_positions
        )
        .reshape(tok_rows, HEAD_SIZE)
        .astype(jnp.bfloat16)
    )
    key_value = jnp.concatenate([key_rot, value_block], axis=1)
    score_scale = 1.0 / math.sqrt(HEAD_SIZE)
    block_part = lax.all_gather(key_value, "zh", axis=0, tiled=False)
    block_part = lax.all_gather(block_part, "y", axis=0, tiled=False)
    block_part = lax.all_to_all(
        jnp.broadcast_to(block_part[None], (lax.axis_size("x"),) + block_part.shape),
        "x",
        0,
        0,
        tiled=True,
    )
    zh_count = block_part.shape[2]
    y_count = block_part.shape[1]
    x_count = block_part.shape[0]
    block_of_key = (
        lax.broadcasted_iota(jnp.int32, (x_count, y_count, zh_count), 2) * (y_count * x_count)
        + lax.broadcasted_iota(jnp.int32, (x_count, y_count, zh_count), 1) * x_count
        + lax.broadcasted_iota(jnp.int32, (x_count, y_count, zh_count), 0)
    )
    key_pos = (
        block_of_key[:, :, :, None] * tok_rows + jnp.arange(tok_rows, dtype=jnp.int32)
    ).reshape(-1)
    block_part = block_part.reshape(-1, 2 * HEAD_SIZE)
    run_max = jnp.broadcast_to(sink_logits[:, None], (local_heads, tok_rows))
    run_total = jnp.ones((local_heads, tok_rows), jnp.float32)
    key_count = block_part.shape[0]
    key_part = block_part[:, :HEAD_SIZE]
    value_part = block_part[:, HEAD_SIZE:].astype(jnp.float32)
    scores = (
        jnp.einsum("rhd,kd->hrk", q_rot, key_part, preferred_element_type=jnp.float32) * score_scale
    )
    visible = token_positions[:, None] >= key_pos[None, :]
    scores = jnp.where(visible[None, :, :], scores, neg_large)
    new_max = jnp.maximum(run_max, jnp.max(scores, axis=2))
    weights = jnp.exp(scores - new_max[:, :, None])
    factor = jnp.exp(run_max - new_max)
    run_total = run_total * factor + jnp.sum(weights, axis=2)
    run_sum = jnp.einsum("hrk,kd->hrd", weights, value_part, precision=lax.Precision.HIGHEST)
    attended = (
        (run_sum / run_total[:, :, None])
        .transpose(1, 0, 2)
        .reshape(tok_rows, local_heads * HEAD_SIZE)
        .astype(jnp.bfloat16)
    )
    head_part = jnp.dot(attended, out_proj, preferred_element_type=jnp.float32).astype(jnp.bfloat16)
    head_part = head_part.reshape(tok_rows, zl_count, c_count, col_width).transpose(2, 1, 0, 3)
    head_part = lax.all_to_all(head_part, "c", split_axis=0, concat_axis=0, tiled=True)
    head_part = jnp.sum(head_part.astype(jnp.float32), axis=0).astype(jnp.bfloat16)
    head_part = lax.all_to_all(head_part, ZL, split_axis=0, concat_axis=0, tiled=True)
    head_cols = jnp.sum(head_part.astype(jnp.float32), axis=0)
    residual_cols = lax.dynamic_slice_in_dim(
        hidden_in, exp_index * col_width, col_width, 1
    ).astype(jnp.float32) + head_cols
    square_part = jnp.sum(residual_cols * residual_cols, axis=1)
    square_high = square_part.astype(jnp.bfloat16)
    square_low = (square_part - square_high.astype(jnp.float32)).astype(jnp.bfloat16)
    gain_cols = lax.dynamic_slice_in_dim(norm_gain, exp_index * col_width, col_width, 0)
    normed_cols = jnp.concatenate(
        [
            (residual_cols * gain_cols[None, :]).astype(jnp.bfloat16),
            square_high[:, None],
            square_low[:, None],
        ],
        axis=1,
    )
    send_width = col_width + 2
    exp_local = gate_up.shape[0]
    n_experts = exp_local * ctx_count
    top_count = expert_ids.shape[1]
    capacity = max(2, tok_rows * top_count * 5 // (4 * n_experts))
    slot_index = route_slots(expert_ids, n_experts)
    dest_row = expert_ids * capacity + slot_index
    spread_rows = jnp.broadcast_to(
        normed_cols[:, None, :], (tok_rows, top_count, send_width)
    ).reshape(tok_rows * top_count, send_width)
    send_rows = (
        jnp.zeros((n_experts * capacity, send_width), jnp.bfloat16)
        .at[dest_row.reshape(-1)]
        .set(spread_rows)
    )
    bucket_rows = ctx_count * capacity
    unit_count = gate_up.shape[-1]
    received = lax.all_to_all(
        send_rows.reshape(ctx_count, exp_local * capacity, send_width),
        CTX,
        split_axis=0,
        concat_axis=0,
        tiled=True,
    ).reshape(bucket_rows, send_width)
    gathered = lax.all_gather(received, ZL, axis=0, tiled=False)
    gathered = lax.all_gather(gathered, "c", axis=0, tiled=False)
    row_squares = jnp.sum(
        gathered[:, :, :, col_width].astype(jnp.float32)
        + gathered[:, :, :, col_width + 1].astype(jnp.float32),
        axis=(0, 1),
    )
    row_scale = lax.rsqrt(row_squares / D + 1e-05)
    weights_flat = gate_up.reshape(zl_count, c_count, col_width, 2 * unit_count)
    gate_up_out = jnp.einsum(
        "czrk,zckf->rf",
        gathered[:, :, :, :col_width],
        weights_flat,
        preferred_element_type=jnp.float32,
    ) * row_scale[:, None]
    gate_up_out = gate_up_out.reshape(bucket_rows, 2, unit_count)
    gate_value = gate_up_out[:, 0]
    up_value = gate_up_out[:, 1]
    activated = ((up_value + 1.0) * gate_value * jax.nn.sigmoid(1.702 * gate_value)).astype(
        jnp.bfloat16
    )
    down_local = down_proj.reshape(unit_count, 2, 2, 2, c_count, col_width)
    partial_value = jnp.einsum(
        "rf,fabecd->cebard", activated, down_local, preferred_element_type=jnp.float32
    ).astype(jnp.bfloat16)
    for axis_name in ("c", "zb0", "zb1"):
        partial_value = lax.all_to_all(partial_value, axis_name, 0, 0, tiled=True)
        partial_value = jnp.sum(partial_value.astype(jnp.float32), axis=0).astype(jnp.bfloat16)
    partial_value = lax.all_to_all(partial_value, "zb2", 0, 0, tiled=True)
    expert_cols = jnp.sum(partial_value.astype(jnp.float32), axis=0).astype(jnp.bfloat16)
    returned = lax.all_to_all(
        expert_cols.reshape(ctx_count, capacity, col_width),
        CTX,
        split_axis=0,
        concat_axis=0,
        tiled=True,
    )
    picked_rows = returned.reshape(n_experts * capacity, col_width)[dest_row]
    moe_cols = jnp.sum(expert_gates[:, :, None] * picked_rows.astype(jnp.float32), axis=1)
    return (residual_cols + moe_cols).astype(jnp.bfloat16)


def solution(mesh):
    ctx_count, exp_count = mesh.devices.shape
    zh, y, x = (mesh.devices.shape[0] // 16, 4, 4)
    c_count = 2
    zl_count = exp_count // c_count
    fine = Mesh(
        mesh.devices.reshape(zh, y, x, 2, 2, 2, c_count),
        ("zh", "y", "x", "zb2", "zb1", "zb0", "c"),
    )
    placed = (
        P(CTX, None),
        P(CTX, EXP),
        P(CTX, None),
        P(CTX, None),
        P(EXP),
        P(EXP, None),
        P(),
        P(CTX, None),
        P(CTX, None),
        P(CTX, None, None, EXP),
        P(CTX, EXP, None),
    )
    return jax.shard_map(
        functools.partial(per_device, ctx_count=ctx_count, zl_count=zl_count, c_count=c_count),
        mesh=fine,
        in_specs=placed,
        out_specs=P(CTX, EXP),
        check_vma=False,
    )
```

```python
import functools
import math

import jax
import jax.numpy as jnp
import numpy as np
from jax import lax
from jax.sharding import Mesh, PartitionSpec as P

D = 2880
QUERY_HEADS = 32
KEY_VALUE_HEADS = 4
HEAD_SIZE = 64


yarn_base = 150000.0
yarn_factor = 32.0
yarn_initial = 4096.0
beta_fast = 32.0
beta_slow = 1.0
neg_large = -1e30


def yarn_frequencies(head_dim):
    half_dim = head_dim // 2

    def correction(rotations):
        return (
            head_dim
            * math.log(yarn_initial / (rotations * 2.0 * math.pi))
            / (2.0 * math.log(yarn_base))
        )

    lower_dim = max(math.floor(correction(beta_fast)), 0)
    upper_dim = min(math.ceil(correction(beta_slow)), head_dim - 1)
    extrap_freq = 1.0 / yarn_base ** (np.arange(0, head_dim, 2) / head_dim)
    interp_freq = extrap_freq / yarn_factor
    ramp_part = np.clip((np.arange(half_dim) - lower_dim) / (upper_dim - lower_dim), 0.0, 1.0)
    extrap_share = 1.0 - ramp_part
    return (interp_freq * (1.0 - extrap_share) + extrap_freq * extrap_share).astype(np.float32)


def rotate_with_yarn(heads_in, token_positions):
    head_dim = heads_in.shape[-1]
    freqs = jnp.asarray(yarn_frequencies(head_dim))
    angles = token_positions.astype(jnp.float32)[:, None] * freqs[None, :]
    factor = 0.1 * math.log(yarn_factor) + 1.0
    cosine = (jnp.cos(angles) * factor)[:, None, :]
    sine = (jnp.sin(angles) * factor)[:, None, :]
    first_half = heads_in[..., : head_dim // 2]
    second_half = heads_in[..., head_dim // 2 :]
    return jnp.concatenate(
        [first_half * cosine - second_half * sine, second_half * cosine + first_half * sine],
        axis=-1,
    )


def route_slots(ids_block, n_experts):
    flat_ids = ids_block.reshape(-1)
    onehot = (flat_ids[:, None] == jnp.arange(n_experts, dtype=jnp.int32)[None, :]).astype(
        jnp.int32
    )
    ranks = jnp.cumsum(onehot, axis=0) - onehot
    return jnp.sum(ranks * onehot, axis=1).reshape(ids_block.shape)


CTX = ("zh", "y", "x")
ZL = ("zlh", "zll")
EXP = ("zlh", "zll", "c")


def per_device(
    hidden_in,
    query_input,
    key_heads_input,
    value_heads_input,
    sink_logits,
    out_proj,
    norm_gain,
    expert_ids,
    expert_gates,
    gate_up,
    down_proj,
    *,
    ctx_count,
    zl_count,
    c_count,
):
    tok_rows = hidden_in.shape[0]
    exp_count = zl_count * c_count
    local_heads = query_input.shape[1] // HEAD_SIZE
    ctx_index = lax.axis_index(CTX)
    exp_index = lax.axis_index(EXP)
    col_width = D // exp_count
    token_positions = ctx_index * tok_rows + jnp.arange(tok_rows, dtype=jnp.int32)
    q_rot = rotate_with_yarn(
        query_input.astype(jnp.float32).reshape(tok_rows, local_heads, HEAD_SIZE), token_positions
    ).astype(jnp.bfloat16)
    shared_key_head = exp_index * local_heads // (QUERY_HEADS // KEY_VALUE_HEADS)
    key_block = lax.dynamic_slice_in_dim(key_heads_input, shared_key_head * HEAD_SIZE, HEAD_SIZE, 1)
    value_block = lax.dynamic_slice_in_dim(
        value_heads_input, shared_key_head * HEAD_SIZE, HEAD_SIZE, 1
    )
    key_rot = (
        rotate_with_yarn(
            key_block.astype(jnp.float32).reshape(tok_rows, 1, HEAD_SIZE), token_positions
        )
        .reshape(tok_rows, HEAD_SIZE)
        .astype(jnp.bfloat16)
    )
    key_value = jnp.concatenate([key_rot, value_block], axis=1)
    score_scale = 1.0 / math.sqrt(HEAD_SIZE)
    block_part = lax.all_gather(key_value, "zh", axis=0, tiled=False)
    block_part = lax.all_gather(block_part, "y", axis=0, tiled=False)
    block_part = lax.all_to_all(
        jnp.broadcast_to(block_part[None], (lax.axis_size("x"),) + block_part.shape),
        "x",
        0,
        0,
        tiled=True,
    )
    zh_count = block_part.shape[2]
    y_count = block_part.shape[1]
    x_count = block_part.shape[0]
    block_of_key = (
        lax.broadcasted_iota(jnp.int32, (x_count, y_count, zh_count), 2) * (y_count * x_count)
        + lax.broadcasted_iota(jnp.int32, (x_count, y_count, zh_count), 1) * x_count
        + lax.broadcasted_iota(jnp.int32, (x_count, y_count, zh_count), 0)
    )
    key_pos = (
        block_of_key[:, :, :, None] * tok_rows + jnp.arange(tok_rows, dtype=jnp.int32)
    ).reshape(-1)
    block_part = block_part.reshape(-1, 2 * HEAD_SIZE)
    run_max = jnp.broadcast_to(sink_logits[:, None], (local_heads, tok_rows))
    run_total = jnp.ones((local_heads, tok_rows), jnp.float32)
    key_count = block_part.shape[0]
    key_part = block_part[:, :HEAD_SIZE]
    value_part = block_part[:, HEAD_SIZE:].astype(jnp.float32)
    scores = (
        jnp.einsum("rhd,kd->hrk", q_rot, key_part, preferred_element_type=jnp.float32) * score_scale
    )
    visible = token_positions[:, None] >= key_pos[None, :]
    scores = jnp.where(visible[None, :, :], scores, neg_large)
    new_max = jnp.maximum(run_max, jnp.max(scores, axis=2))
    weights = jnp.exp(scores - new_max[:, :, None])
    factor = jnp.exp(run_max - new_max)
    run_total = run_total * factor + jnp.sum(weights, axis=2)
    run_sum = jnp.einsum("hrk,kd->hrd", weights, value_part, precision=lax.Precision.HIGHEST)
    attended = (
        (run_sum / run_total[:, :, None])
        .transpose(1, 0, 2)
        .reshape(tok_rows, local_heads * HEAD_SIZE)
        .astype(jnp.bfloat16)
    )
    head_part = jnp.dot(attended, out_proj, preferred_element_type=jnp.float32).astype(jnp.bfloat16)
    head_part = head_part.reshape(tok_rows, zl_count, c_count, col_width).transpose(2, 1, 0, 3)
    head_part = lax.all_to_all(head_part, "c", split_axis=0, concat_axis=0, tiled=True)
    head_part = jnp.sum(head_part.astype(jnp.float32), axis=0).astype(jnp.bfloat16)
    head_part = lax.all_to_all(head_part, ZL, split_axis=0, concat_axis=0, tiled=True)
    head_cols = jnp.sum(head_part.astype(jnp.float32), axis=0)
    residual_cols = lax.dynamic_slice_in_dim(
        hidden_in, exp_index * col_width, col_width, 1
    ).astype(jnp.float32) + head_cols
    square_part = jnp.sum(residual_cols * residual_cols, axis=1)
    square_high = square_part.astype(jnp.bfloat16)
    square_low = (square_part - square_high.astype(jnp.float32)).astype(jnp.bfloat16)
    gain_cols = lax.dynamic_slice_in_dim(norm_gain, exp_index * col_width, col_width, 0)
    normed_cols = jnp.concatenate(
        [
            (residual_cols * gain_cols[None, :]).astype(jnp.bfloat16),
            square_high[:, None],
            square_low[:, None],
        ],
        axis=1,
    )
    send_width = col_width + 2
    exp_local = gate_up.shape[0]
    n_experts = exp_local * ctx_count
    top_count = expert_ids.shape[1]
    capacity = max(2, tok_rows * top_count * 5 // (4 * n_experts))
    slot_index = route_slots(expert_ids, n_experts)
    dest_row = expert_ids * capacity + slot_index
    spread_rows = jnp.broadcast_to(
        normed_cols[:, None, :], (tok_rows, top_count, send_width)
    ).reshape(tok_rows * top_count, send_width)
    send_rows = (
        jnp.zeros((n_experts * capacity, send_width), jnp.bfloat16)
        .at[dest_row.reshape(-1)]
        .set(spread_rows)
    )
    bucket_rows = ctx_count * capacity
    unit_count = gate_up.shape[-1]
    received = lax.all_to_all(
        send_rows.reshape(ctx_count, exp_local * capacity, send_width),
        CTX,
        split_axis=0,
        concat_axis=0,
        tiled=True,
    ).reshape(bucket_rows, send_width)
    gathered = lax.all_gather(received, ZL, axis=0, tiled=False)
    gathered = lax.all_gather(gathered, "c", axis=0, tiled=False)
    row_squares = jnp.sum(
        gathered[:, :, :, col_width].astype(jnp.float32)
        + gathered[:, :, :, col_width + 1].astype(jnp.float32),
        axis=(0, 1),
    )
    row_scale = lax.rsqrt(row_squares / D + 1e-05)
    weights_flat = gate_up.reshape(zl_count, c_count, col_width, 2 * unit_count)
    gate_up_out = jnp.einsum(
        "czrk,zckf->rf",
        gathered[:, :, :, :col_width],
        weights_flat,
        preferred_element_type=jnp.float32,
    ) * row_scale[:, None]
    gate_up_out = gate_up_out.reshape(bucket_rows, 2, unit_count)
    gate_value = gate_up_out[:, 0]
    up_value = gate_up_out[:, 1]
    activated = ((up_value + 1.0) * gate_value * jax.nn.sigmoid(1.702 * gate_value)).astype(
        jnp.bfloat16
    )
    zlh_count = zl_count // 2
    down_local = down_proj.reshape(unit_count, zlh_count, 2, c_count, col_width)
    partial_value = jnp.einsum(
        "rf,fhlcd->chlrd", activated, down_local, preferred_element_type=jnp.float32
    ).astype(jnp.bfloat16)
    partial_value = lax.all_to_all(partial_value, "c", 0, 0, tiled=True)
    partial_value = jnp.sum(partial_value.astype(jnp.float32), axis=0).astype(jnp.bfloat16)
    partial_value = lax.all_to_all(partial_value.transpose(1, 0, 2, 3), "zll", 0, 0, tiled=True)
    partial_value = jnp.sum(partial_value.astype(jnp.float32), axis=0).astype(jnp.bfloat16)
    partial_value = lax.all_to_all(partial_value, "zlh", 0, 0, tiled=True)
    expert_cols = jnp.sum(partial_value.astype(jnp.float32), axis=0).astype(jnp.bfloat16)
    returned = lax.all_to_all(
        expert_cols.reshape(ctx_count, capacity, col_width),
        CTX,
        split_axis=0,
        concat_axis=0,
        tiled=True,
    )
    picked_rows = returned.reshape(n_experts * capacity, col_width)[dest_row]
    moe_cols = jnp.sum(expert_gates[:, :, None] * picked_rows.astype(jnp.float32), axis=1)
    return (residual_cols + moe_cols).astype(jnp.bfloat16)


def solution(mesh):
    ctx_count, exp_count = mesh.devices.shape
    zh, y, x = (mesh.devices.shape[0] // 16, 4, 4)
    c_count = 2
    zl_count = exp_count // c_count
    fine = Mesh(
        mesh.devices.reshape(zh, y, x, zl_count // 2, 2, c_count), ("zh", "y", "x", "zlh", "zll", "c")
    )
    placed = (
        P(CTX, None),
        P(CTX, EXP),
        P(CTX, None),
        P(CTX, None),
        P(EXP),
        P(EXP, None),
        P(),
        P(CTX, None),
        P(CTX, None),
        P(CTX, None, None, EXP),
        P(CTX, EXP, None),
    )
    return jax.shard_map(
        functools.partial(per_device, ctx_count=ctx_count, zl_count=zl_count, c_count=c_count),
        mesh=fine,
        in_specs=placed,
        out_specs=P(CTX, EXP),
        check_vma=False,
    )
```

```python
import functools
import math

import jax
import jax.numpy as jnp
import numpy as np
from jax import lax
from jax.sharding import Mesh, PartitionSpec as P

D = 2880
QUERY_HEADS = 32
KEY_VALUE_HEADS = 4
HEAD_SIZE = 64


yarn_base = 150000.0
yarn_factor = 32.0
yarn_initial = 4096.0
beta_fast = 32.0
beta_slow = 1.0
neg_large = -1e30


def yarn_frequencies(head_dim):
    half_dim = head_dim // 2

    def correction(rotations):
        return (
            head_dim
            * math.log(yarn_initial / (rotations * 2.0 * math.pi))
            / (2.0 * math.log(yarn_base))
        )

    lower_dim = max(math.floor(correction(beta_fast)), 0)
    upper_dim = min(math.ceil(correction(beta_slow)), head_dim - 1)
    extrap_freq = 1.0 / yarn_base ** (np.arange(0, head_dim, 2) / head_dim)
    interp_freq = extrap_freq / yarn_factor
    ramp_part = np.clip((np.arange(half_dim) - lower_dim) / (upper_dim - lower_dim), 0.0, 1.0)
    extrap_share = 1.0 - ramp_part
    return (interp_freq * (1.0 - extrap_share) + extrap_freq * extrap_share).astype(np.float32)


def rotate_with_yarn(heads_in, token_positions):
    head_dim = heads_in.shape[-1]
    freqs = jnp.asarray(yarn_frequencies(head_dim))
    angles = token_positions.astype(jnp.float32)[:, None] * freqs[None, :]
    factor = 0.1 * math.log(yarn_factor) + 1.0
    cosine = (jnp.cos(angles) * factor)[:, None, :]
    sine = (jnp.sin(angles) * factor)[:, None, :]
    first_half = heads_in[..., : head_dim // 2]
    second_half = heads_in[..., head_dim // 2 :]
    return jnp.concatenate(
        [first_half * cosine - second_half * sine, second_half * cosine + first_half * sine],
        axis=-1,
    )


def route_slots(ids_block, n_experts):
    flat_ids = ids_block.reshape(-1)
    onehot = (flat_ids[:, None] == jnp.arange(n_experts, dtype=jnp.int32)[None, :]).astype(
        jnp.int32
    )
    ranks = jnp.cumsum(onehot, axis=0) - onehot
    return jnp.sum(ranks * onehot, axis=1).reshape(ids_block.shape)


CTX = ("zh", "y", "x")
ZL = ("zlh", "zll")
EXP = ("zlh", "zll", "c")


def per_device(
    hidden_in,
    query_input,
    key_heads_input,
    value_heads_input,
    sink_logits,
    out_proj,
    norm_gain,
    expert_ids,
    expert_gates,
    gate_up,
    down_proj,
    *,
    ctx_count,
    zl_count,
    c_count,
):
    tok_rows = hidden_in.shape[0]
    exp_count = zl_count * c_count
    local_heads = query_input.shape[1] // HEAD_SIZE
    ctx_index = lax.axis_index(CTX)
    exp_index = lax.axis_index(EXP)
    col_width = D // exp_count
    token_positions = ctx_index * tok_rows + jnp.arange(tok_rows, dtype=jnp.int32)
    q_rot = rotate_with_yarn(
        query_input.astype(jnp.float32).reshape(tok_rows, local_heads, HEAD_SIZE), token_positions
    ).astype(jnp.bfloat16)
    shared_key_head = exp_index * local_heads // (QUERY_HEADS // KEY_VALUE_HEADS)
    key_block = lax.dynamic_slice_in_dim(key_heads_input, shared_key_head * HEAD_SIZE, HEAD_SIZE, 1)
    value_block = lax.dynamic_slice_in_dim(
        value_heads_input, shared_key_head * HEAD_SIZE, HEAD_SIZE, 1
    )
    key_rot = (
        rotate_with_yarn(
            key_block.astype(jnp.float32).reshape(tok_rows, 1, HEAD_SIZE), token_positions
        )
        .reshape(tok_rows, HEAD_SIZE)
        .astype(jnp.bfloat16)
    )
    key_value = jnp.concatenate([key_rot, value_block], axis=1)
    score_scale = 1.0 / math.sqrt(HEAD_SIZE)
    block_part = key_value
    for axis_name in ("zh", "y"):
        block_part = lax.all_to_all(
            jnp.broadcast_to(block_part[None], (lax.axis_size(axis_name),) + block_part.shape),
            axis_name,
            0,
            0,
            tiled=True,
        )
    block_part = lax.all_to_all(
        jnp.broadcast_to(block_part[None], (lax.axis_size("x"),) + block_part.shape),
        "x",
        0,
        0,
        tiled=True,
    )
    zh_count = block_part.shape[2]
    y_count = block_part.shape[1]
    x_count = block_part.shape[0]
    block_of_key = (
        lax.broadcasted_iota(jnp.int32, (x_count, y_count, zh_count), 2) * (y_count * x_count)
        + lax.broadcasted_iota(jnp.int32, (x_count, y_count, zh_count), 1) * x_count
        + lax.broadcasted_iota(jnp.int32, (x_count, y_count, zh_count), 0)
    )
    key_pos = (
        block_of_key[:, :, :, None] * tok_rows + jnp.arange(tok_rows, dtype=jnp.int32)
    ).reshape(-1)
    block_part = block_part.reshape(-1, 2 * HEAD_SIZE)
    run_max = jnp.broadcast_to(sink_logits[:, None], (local_heads, tok_rows))
    run_total = jnp.ones((local_heads, tok_rows), jnp.float32)
    key_count = block_part.shape[0]
    key_part = block_part[:, :HEAD_SIZE]
    value_part = block_part[:, HEAD_SIZE:].astype(jnp.float32)
    scores = (
        jnp.einsum("rhd,kd->hrk", q_rot, key_part, preferred_element_type=jnp.float32) * score_scale
    )
    visible = token_positions[:, None] >= key_pos[None, :]
    scores = jnp.where(visible[None, :, :], scores, neg_large)
    new_max = jnp.maximum(run_max, jnp.max(scores, axis=2))
    weights = jnp.exp(scores - new_max[:, :, None])
    factor = jnp.exp(run_max - new_max)
    run_total = run_total * factor + jnp.sum(weights, axis=2)
    run_sum = jnp.einsum("hrk,kd->hrd", weights, value_part, precision=lax.Precision.HIGHEST)
    attended = (
        (run_sum / run_total[:, :, None])
        .transpose(1, 0, 2)
        .reshape(tok_rows, local_heads * HEAD_SIZE)
        .astype(jnp.bfloat16)
    )
    head_part = jnp.dot(attended, out_proj, preferred_element_type=jnp.float32).astype(jnp.bfloat16)
    head_part = head_part.reshape(tok_rows, zl_count, c_count, col_width).transpose(2, 1, 0, 3)
    head_part = lax.all_to_all(head_part, "c", split_axis=0, concat_axis=0, tiled=True)
    head_part = jnp.sum(head_part.astype(jnp.float32), axis=0).astype(jnp.bfloat16)
    head_part = lax.all_to_all(head_part, ZL, split_axis=0, concat_axis=0, tiled=True)
    head_cols = jnp.sum(head_part.astype(jnp.float32), axis=0)
    residual_cols = lax.dynamic_slice_in_dim(
        hidden_in, exp_index * col_width, col_width, 1
    ).astype(jnp.float32) + head_cols
    square_part = jnp.sum(residual_cols * residual_cols, axis=1)
    square_high = square_part.astype(jnp.bfloat16)
    square_low = (square_part - square_high.astype(jnp.float32)).astype(jnp.bfloat16)
    gain_cols = lax.dynamic_slice_in_dim(norm_gain, exp_index * col_width, col_width, 0)
    normed_cols = jnp.concatenate(
        [
            (residual_cols * gain_cols[None, :]).astype(jnp.bfloat16),
            square_high[:, None],
            square_low[:, None],
        ],
        axis=1,
    )
    send_width = col_width + 2
    exp_local = gate_up.shape[0]
    n_experts = exp_local * ctx_count
    top_count = expert_ids.shape[1]
    capacity = max(2, tok_rows * top_count * 5 // (4 * n_experts))
    slot_index = route_slots(expert_ids, n_experts)
    dest_row = expert_ids * capacity + slot_index
    spread_rows = jnp.broadcast_to(
        normed_cols[:, None, :], (tok_rows, top_count, send_width)
    ).reshape(tok_rows * top_count, send_width)
    send_rows = (
        jnp.zeros((n_experts * capacity, send_width), jnp.bfloat16)
        .at[dest_row.reshape(-1)]
        .set(spread_rows)
    )
    bucket_rows = ctx_count * capacity
    unit_count = gate_up.shape[-1]
    received = lax.all_to_all(
        send_rows.reshape(ctx_count, exp_local * capacity, send_width),
        CTX,
        split_axis=0,
        concat_axis=0,
        tiled=True,
    ).reshape(bucket_rows, send_width)
    gathered = lax.all_gather(received, ZL, axis=0, tiled=False)
    gathered = lax.all_gather(gathered, "c", axis=0, tiled=False)
    row_squares = jnp.sum(
        gathered[:, :, :, col_width].astype(jnp.float32)
        + gathered[:, :, :, col_width + 1].astype(jnp.float32),
        axis=(0, 1),
    )
    row_scale = lax.rsqrt(row_squares / D + 1e-05)
    weights_flat = gate_up.reshape(zl_count, c_count, col_width, 2 * unit_count)
    gate_up_out = jnp.einsum(
        "czrk,zckf->rf",
        gathered[:, :, :, :col_width],
        weights_flat,
        preferred_element_type=jnp.float32,
    ) * row_scale[:, None]
    gate_up_out = gate_up_out.reshape(bucket_rows, 2, unit_count)
    gate_value = gate_up_out[:, 0]
    up_value = gate_up_out[:, 1]
    activated = ((up_value + 1.0) * gate_value * jax.nn.sigmoid(1.702 * gate_value)).astype(
        jnp.bfloat16
    )
    zlh_count = zl_count // 2
    down_local = down_proj.reshape(unit_count, zlh_count, 2, c_count, col_width)
    partial_value = jnp.einsum(
        "rf,fhlcd->chlrd", activated, down_local, preferred_element_type=jnp.float32
    ).astype(jnp.bfloat16)
    partial_value = lax.all_to_all(partial_value, "c", 0, 0, tiled=True)
    partial_value = jnp.sum(partial_value.astype(jnp.float32), axis=0).astype(jnp.bfloat16)
    partial_value = lax.all_to_all(partial_value.transpose(1, 0, 2, 3), "zll", 0, 0, tiled=True)
    partial_value = jnp.sum(partial_value.astype(jnp.float32), axis=0).astype(jnp.bfloat16)
    partial_value = lax.all_to_all(partial_value, "zlh", 0, 0, tiled=True)
    expert_cols = jnp.sum(partial_value.astype(jnp.float32), axis=0).astype(jnp.bfloat16)
    returned = lax.all_to_all(
        expert_cols.reshape(ctx_count, capacity, col_width),
        CTX,
        split_axis=0,
        concat_axis=0,
        tiled=True,
    )
    picked_rows = returned.reshape(n_experts * capacity, col_width)[dest_row]
    moe_cols = jnp.sum(expert_gates[:, :, None] * picked_rows.astype(jnp.float32), axis=1)
    return (residual_cols + moe_cols).astype(jnp.bfloat16)


def solution(mesh):
    ctx_count, exp_count = mesh.devices.shape
    zh, y, x = (mesh.devices.shape[0] // 16, 4, 4)
    c_count = 2
    zl_count = exp_count // c_count
    fine = Mesh(
        mesh.devices.reshape(zh, y, x, zl_count // 2, 2, c_count), ("zh", "y", "x", "zlh", "zll", "c")
    )
    placed = (
        P(CTX, None),
        P(CTX, EXP),
        P(CTX, None),
        P(CTX, None),
        P(EXP),
        P(EXP, None),
        P(),
        P(CTX, None),
        P(CTX, None),
        P(CTX, None, None, EXP),
        P(CTX, EXP, None),
    )
    return jax.shard_map(
        functools.partial(per_device, ctx_count=ctx_count, zl_count=zl_count, c_count=c_count),
        mesh=fine,
        in_specs=placed,
        out_specs=P(CTX, EXP),
        check_vma=False,
    )
```

```python
import functools
import math

import jax
import jax.numpy as jnp
import numpy as np
from jax import lax
from jax.sharding import Mesh, PartitionSpec as P

D = 2880
QUERY_HEADS = 32
KEY_VALUE_HEADS = 4
HEAD_SIZE = 64


yarn_base = 150000.0
yarn_factor = 32.0
yarn_initial = 4096.0
beta_fast = 32.0
beta_slow = 1.0
neg_large = -1e30


def yarn_frequencies(head_dim):
    half_dim = head_dim // 2

    def correction(rotations):
        return (
            head_dim
            * math.log(yarn_initial / (rotations * 2.0 * math.pi))
            / (2.0 * math.log(yarn_base))
        )

    lower_dim = max(math.floor(correction(beta_fast)), 0)
    upper_dim = min(math.ceil(correction(beta_slow)), head_dim - 1)
    extrap_freq = 1.0 / yarn_base ** (np.arange(0, head_dim, 2) / head_dim)
    interp_freq = extrap_freq / yarn_factor
    ramp_part = np.clip((np.arange(half_dim) - lower_dim) / (upper_dim - lower_dim), 0.0, 1.0)
    extrap_share = 1.0 - ramp_part
    return (interp_freq * (1.0 - extrap_share) + extrap_freq * extrap_share).astype(np.float32)


def rotate_with_yarn(heads_in, token_positions):
    head_dim = heads_in.shape[-1]
    freqs = jnp.asarray(yarn_frequencies(head_dim))
    angles = token_positions.astype(jnp.float32)[:, None] * freqs[None, :]
    factor = 0.1 * math.log(yarn_factor) + 1.0
    cosine = (jnp.cos(angles) * factor)[:, None, :]
    sine = (jnp.sin(angles) * factor)[:, None, :]
    first_half = heads_in[..., : head_dim // 2]
    second_half = heads_in[..., head_dim // 2 :]
    return jnp.concatenate(
        [first_half * cosine - second_half * sine, second_half * cosine + first_half * sine],
        axis=-1,
    )


def route_slots(ids_block, n_experts):
    flat_ids = ids_block.reshape(-1)
    onehot = (flat_ids[:, None] == jnp.arange(n_experts, dtype=jnp.int32)[None, :]).astype(
        jnp.int32
    )
    ranks = jnp.cumsum(onehot, axis=0) - onehot
    return jnp.sum(ranks * onehot, axis=1).reshape(ids_block.shape)


CTX = ("zh", "y", "x")
ZL = ("zlh", "zll")
EXP = ("zlh", "zll", "c")


def per_device(
    hidden_in,
    query_input,
    key_heads_input,
    value_heads_input,
    sink_logits,
    out_proj,
    norm_gain,
    expert_ids,
    expert_gates,
    gate_up,
    down_proj,
    *,
    ctx_count,
    zl_count,
    c_count,
):
    tok_rows = hidden_in.shape[0]
    exp_count = zl_count * c_count
    local_heads = query_input.shape[1] // HEAD_SIZE
    ctx_index = lax.axis_index(CTX)
    exp_index = lax.axis_index(EXP)
    col_width = D // exp_count
    token_positions = ctx_index * tok_rows + jnp.arange(tok_rows, dtype=jnp.int32)
    q_rot = rotate_with_yarn(
        query_input.astype(jnp.float32).reshape(tok_rows, local_heads, HEAD_SIZE), token_positions
    ).astype(jnp.bfloat16)
    shared_key_head = exp_index * local_heads // (QUERY_HEADS // KEY_VALUE_HEADS)
    key_block = lax.dynamic_slice_in_dim(key_heads_input, shared_key_head * HEAD_SIZE, HEAD_SIZE, 1)
    value_block = lax.dynamic_slice_in_dim(
        value_heads_input, shared_key_head * HEAD_SIZE, HEAD_SIZE, 1
    )
    key_rot = (
        rotate_with_yarn(
            key_block.astype(jnp.float32).reshape(tok_rows, 1, HEAD_SIZE), token_positions
        )
        .reshape(tok_rows, HEAD_SIZE)
        .astype(jnp.bfloat16)
    )
    key_value = jnp.concatenate([key_rot, value_block], axis=1)
    score_scale = 1.0 / math.sqrt(HEAD_SIZE)
    block_part = lax.all_gather(key_value, "zh", axis=0, tiled=False)
    block_part = lax.all_gather(block_part, "y", axis=0, tiled=False)
    block_part = lax.all_to_all(
        jnp.broadcast_to(block_part[None], (lax.axis_size("x"),) + block_part.shape),
        "x",
        0,
        0,
        tiled=True,
    )
    zh_count = block_part.shape[2]
    y_count = block_part.shape[1]
    x_count = block_part.shape[0]
    block_of_key = (
        lax.broadcasted_iota(jnp.int32, (x_count, y_count, zh_count), 2) * (y_count * x_count)
        + lax.broadcasted_iota(jnp.int32, (x_count, y_count, zh_count), 1) * x_count
        + lax.broadcasted_iota(jnp.int32, (x_count, y_count, zh_count), 0)
    )
    key_pos = (
        block_of_key[:, :, :, None] * tok_rows + jnp.arange(tok_rows, dtype=jnp.int32)
    ).reshape(-1)
    block_part = block_part.reshape(-1, 2 * HEAD_SIZE)
    run_max = jnp.broadcast_to(sink_logits[:, None], (local_heads, tok_rows))
    run_total = jnp.ones((local_heads, tok_rows), jnp.float32)
    key_count = block_part.shape[0]
    key_part = block_part[:, :HEAD_SIZE]
    value_part = block_part[:, HEAD_SIZE:].astype(jnp.float32)
    scores = (
        jnp.einsum("rhd,kd->hrk", q_rot, key_part, preferred_element_type=jnp.float32) * score_scale
    )
    visible = token_positions[:, None] >= key_pos[None, :]
    scores = jnp.where(visible[None, :, :], scores, neg_large)
    new_max = jnp.maximum(run_max, jnp.max(scores, axis=2))
    weights = jnp.exp(scores - new_max[:, :, None])
    factor = jnp.exp(run_max - new_max)
    run_total = run_total * factor + jnp.sum(weights, axis=2)
    run_sum = jnp.einsum("hrk,kd->hrd", weights, value_part, precision=lax.Precision.HIGHEST)
    attended = (
        (run_sum / run_total[:, :, None])
        .transpose(1, 0, 2)
        .reshape(tok_rows, local_heads * HEAD_SIZE)
        .astype(jnp.bfloat16)
    )
    head_part = jnp.dot(attended, out_proj, preferred_element_type=jnp.float32).astype(jnp.bfloat16)
    head_part = head_part.reshape(tok_rows, zl_count, c_count, col_width).transpose(2, 1, 0, 3)
    head_part = lax.all_to_all(head_part, "c", split_axis=0, concat_axis=0, tiled=True)
    head_part = jnp.sum(head_part.astype(jnp.float32), axis=0).astype(jnp.bfloat16)
    head_part = lax.all_to_all(head_part, ZL, split_axis=0, concat_axis=0, tiled=True)
    head_cols = jnp.sum(head_part.astype(jnp.float32), axis=0)
    residual_cols = lax.dynamic_slice_in_dim(
        hidden_in, exp_index * col_width, col_width, 1
    ).astype(jnp.float32) + head_cols
    square_part = jnp.sum(residual_cols * residual_cols, axis=1)
    square_high = square_part.astype(jnp.bfloat16)
    square_low = (square_part - square_high.astype(jnp.float32)).astype(jnp.bfloat16)
    gain_cols = lax.dynamic_slice_in_dim(norm_gain, exp_index * col_width, col_width, 0)
    normed_cols = jnp.concatenate(
        [
            (residual_cols * gain_cols[None, :]).astype(jnp.bfloat16),
            square_high[:, None],
            square_low[:, None],
        ],
        axis=1,
    )
    send_width = col_width + 2
    exp_local = gate_up.shape[0]
    n_experts = exp_local * ctx_count
    top_count = expert_ids.shape[1]
    capacity = max(2, tok_rows * top_count * 5 // (4 * n_experts))
    slot_index = route_slots(expert_ids, n_experts)
    dest_row = expert_ids * capacity + slot_index
    spread_rows = jnp.broadcast_to(
        normed_cols[:, None, :], (tok_rows, top_count, send_width)
    ).reshape(tok_rows * top_count, send_width)
    send_rows = (
        jnp.zeros((n_experts * capacity, send_width), jnp.bfloat16)
        .at[dest_row.reshape(-1)]
        .set(spread_rows)
    )
    bucket_rows = ctx_count * capacity
    unit_count = gate_up.shape[-1]
    received = lax.all_to_all(
        send_rows.reshape(ctx_count, exp_local * capacity, send_width),
        CTX,
        split_axis=0,
        concat_axis=0,
        tiled=True,
    ).reshape(bucket_rows, send_width)
    gathered = lax.all_gather(received, ZL, axis=0, tiled=False)
    gathered = lax.all_gather(gathered, "c", axis=0, tiled=False)
    row_squares = jnp.sum(
        gathered[:, :, :, col_width].astype(jnp.float32)
        + gathered[:, :, :, col_width + 1].astype(jnp.float32),
        axis=(0, 1),
    )
    row_scale = lax.rsqrt(row_squares / D + 1e-05)
    weights_flat = gate_up.reshape(zl_count, c_count, col_width, 2 * unit_count)
    gate_up_out = jnp.einsum(
        "czrk,zckf->rf",
        gathered[:, :, :, :col_width],
        weights_flat,
        preferred_element_type=jnp.float32,
    ) * row_scale[:, None]
    gate_up_out = gate_up_out.reshape(bucket_rows, 2, unit_count)
    gate_value = gate_up_out[:, 0]
    up_value = gate_up_out[:, 1]
    activated = ((up_value + 1.0) * gate_value * jax.nn.sigmoid(1.702 * gate_value)).astype(
        jnp.bfloat16
    )
    zlh_count = zl_count // 2
    down_local = down_proj.reshape(unit_count, zlh_count, 2, c_count, col_width)
    partial_value = jnp.einsum(
        "rf,fhlcd->chlrd", activated, down_local, preferred_element_type=jnp.float32
    ).astype(jnp.bfloat16)
    partial_value = lax.all_to_all(partial_value, "c", 0, 0, tiled=True)
    partial_value = jnp.sum(partial_value.astype(jnp.float32), axis=0).astype(jnp.bfloat16)
    partial_value = lax.all_to_all(partial_value.transpose(1, 0, 2, 3), "zll", 0, 0, tiled=True)
    partial_value = jnp.sum(partial_value.astype(jnp.float32), axis=0).astype(jnp.bfloat16)
    expert_cols = lax.psum_scatter(partial_value, "zlh", scatter_dimension=0, tiled=True)[0]
    returned = lax.all_to_all(
        expert_cols.reshape(ctx_count, capacity, col_width),
        CTX,
        split_axis=0,
        concat_axis=0,
        tiled=True,
    )
    picked_rows = returned.reshape(n_experts * capacity, col_width)[dest_row]
    moe_cols = jnp.sum(expert_gates[:, :, None] * picked_rows.astype(jnp.float32), axis=1)
    return (residual_cols + moe_cols).astype(jnp.bfloat16)


def solution(mesh):
    ctx_count, exp_count = mesh.devices.shape
    zh, y, x = (mesh.devices.shape[0] // 16, 4, 4)
    c_count = 2
    zl_count = exp_count // c_count
    fine = Mesh(
        mesh.devices.reshape(zh, y, x, zl_count // 2, 2, c_count), ("zh", "y", "x", "zlh", "zll", "c")
    )
    placed = (
        P(CTX, None),
        P(CTX, EXP),
        P(CTX, None),
        P(CTX, None),
        P(EXP),
        P(EXP, None),
        P(),
        P(CTX, None),
        P(CTX, None),
        P(CTX, None, None, EXP),
        P(CTX, EXP, None),
    )
    return jax.shard_map(
        functools.partial(per_device, ctx_count=ctx_count, zl_count=zl_count, c_count=c_count),
        mesh=fine,
        in_specs=placed,
        out_specs=P(CTX, EXP),
        check_vma=False,
    )
```

```python
import functools
import math

import jax
import jax.numpy as jnp
import numpy as np
from jax import lax
from jax.sharding import Mesh, PartitionSpec as P

D = 2880
QUERY_HEADS = 32
KEY_VALUE_HEADS = 4
HEAD_SIZE = 64


yarn_base = 150000.0
yarn_factor = 32.0
yarn_initial = 4096.0
beta_fast = 32.0
beta_slow = 1.0
neg_large = -1e30


def yarn_frequencies(head_dim):
    half_dim = head_dim // 2

    def correction(rotations):
        return (
            head_dim
            * math.log(yarn_initial / (rotations * 2.0 * math.pi))
            / (2.0 * math.log(yarn_base))
        )

    lower_dim = max(math.floor(correction(beta_fast)), 0)
    upper_dim = min(math.ceil(correction(beta_slow)), head_dim - 1)
    extrap_freq = 1.0 / yarn_base ** (np.arange(0, head_dim, 2) / head_dim)
    interp_freq = extrap_freq / yarn_factor
    ramp_part = np.clip((np.arange(half_dim) - lower_dim) / (upper_dim - lower_dim), 0.0, 1.0)
    extrap_share = 1.0 - ramp_part
    return (interp_freq * (1.0 - extrap_share) + extrap_freq * extrap_share).astype(np.float32)


def rotate_with_yarn(heads_in, token_positions):
    head_dim = heads_in.shape[-1]
    freqs = jnp.asarray(yarn_frequencies(head_dim))
    angles = token_positions.astype(jnp.float32)[:, None] * freqs[None, :]
    factor = 0.1 * math.log(yarn_factor) + 1.0
    cosine = (jnp.cos(angles) * factor)[:, None, :]
    sine = (jnp.sin(angles) * factor)[:, None, :]
    first_half = heads_in[..., : head_dim // 2]
    second_half = heads_in[..., head_dim // 2 :]
    return jnp.concatenate(
        [first_half * cosine - second_half * sine, second_half * cosine + first_half * sine],
        axis=-1,
    )


def route_slots(ids_block, n_experts):
    flat_ids = ids_block.reshape(-1)
    onehot = (flat_ids[:, None] == jnp.arange(n_experts, dtype=jnp.int32)[None, :]).astype(
        jnp.int32
    )
    ranks = jnp.cumsum(onehot, axis=0) - onehot
    return jnp.sum(ranks * onehot, axis=1).reshape(ids_block.shape)


CTX = ("zh", "y", "x")
ZL = ("zlh", "zll")
EXP = ("zlh", "zll", "c")


def per_device(
    hidden_in,
    query_input,
    key_heads_input,
    value_heads_input,
    sink_logits,
    out_proj,
    norm_gain,
    expert_ids,
    expert_gates,
    gate_up,
    down_proj,
    *,
    ctx_count,
    zl_count,
    c_count,
):
    tok_rows = hidden_in.shape[0]
    exp_count = zl_count * c_count
    local_heads = query_input.shape[1] // HEAD_SIZE
    ctx_index = lax.axis_index(CTX)
    exp_index = lax.axis_index(EXP)
    col_width = D // exp_count
    token_positions = ctx_index * tok_rows + jnp.arange(tok_rows, dtype=jnp.int32)
    q_rot = rotate_with_yarn(
        query_input.astype(jnp.float32).reshape(tok_rows, local_heads, HEAD_SIZE), token_positions
    ).astype(jnp.bfloat16)
    shared_key_head = exp_index * local_heads // (QUERY_HEADS // KEY_VALUE_HEADS)
    key_block = lax.dynamic_slice_in_dim(key_heads_input, shared_key_head * HEAD_SIZE, HEAD_SIZE, 1)
    value_block = lax.dynamic_slice_in_dim(
        value_heads_input, shared_key_head * HEAD_SIZE, HEAD_SIZE, 1
    )
    key_rot = (
        rotate_with_yarn(
            key_block.astype(jnp.float32).reshape(tok_rows, 1, HEAD_SIZE), token_positions
        )
        .reshape(tok_rows, HEAD_SIZE)
        .astype(jnp.bfloat16)
    )
    key_value = jnp.concatenate([key_rot, value_block], axis=1)
    score_scale = 1.0 / math.sqrt(HEAD_SIZE)
    block_part = lax.all_gather(key_value, "zh", axis=0, tiled=False)
    block_part = lax.all_gather(block_part, "y", axis=0, tiled=False)
    block_part = lax.all_to_all(
        jnp.broadcast_to(block_part[None], (lax.axis_size("x"),) + block_part.shape),
        "x",
        0,
        0,
        tiled=True,
    )
    zh_count = block_part.shape[2]
    y_count = block_part.shape[1]
    x_count = block_part.shape[0]
    block_of_key = (
        lax.broadcasted_iota(jnp.int32, (x_count, y_count, zh_count), 2) * (y_count * x_count)
        + lax.broadcasted_iota(jnp.int32, (x_count, y_count, zh_count), 1) * x_count
        + lax.broadcasted_iota(jnp.int32, (x_count, y_count, zh_count), 0)
    )
    key_pos = (
        block_of_key[:, :, :, None] * tok_rows + jnp.arange(tok_rows, dtype=jnp.int32)
    ).reshape(-1)
    block_part = block_part.reshape(-1, 2 * HEAD_SIZE)
    run_max = jnp.broadcast_to(sink_logits[:, None], (local_heads, tok_rows))
    run_total = jnp.ones((local_heads, tok_rows), jnp.float32)
    key_count = block_part.shape[0]
    key_part = block_part[:, :HEAD_SIZE]
    value_part = block_part[:, HEAD_SIZE:].astype(jnp.float32)
    scores = (
        jnp.einsum("rhd,kd->hrk", q_rot, key_part, preferred_element_type=jnp.float32) * score_scale
    )
    visible = token_positions[:, None] >= key_pos[None, :]
    scores = jnp.where(visible[None, :, :], scores, neg_large)
    new_max = jnp.maximum(run_max, jnp.max(scores, axis=2))
    weights = jnp.exp(scores - new_max[:, :, None])
    factor = jnp.exp(run_max - new_max)
    run_total = run_total * factor + jnp.sum(weights, axis=2)
    run_sum = jnp.einsum("hrk,kd->hrd", weights, value_part, precision=lax.Precision.HIGHEST)
    attended = (
        (run_sum / run_total[:, :, None])
        .transpose(1, 0, 2)
        .reshape(tok_rows, local_heads * HEAD_SIZE)
        .astype(jnp.bfloat16)
    )
    head_part = jnp.dot(attended, out_proj, preferred_element_type=jnp.float32).astype(jnp.bfloat16)
    head_part = head_part.reshape(tok_rows, zl_count, c_count, col_width).transpose(2, 1, 0, 3)
    head_part = lax.all_to_all(head_part, "c", split_axis=0, concat_axis=0, tiled=True)
    head_part = jnp.sum(head_part.astype(jnp.float32), axis=0).astype(jnp.bfloat16)
    head_part = lax.all_to_all(head_part, ZL, split_axis=0, concat_axis=0, tiled=True)
    head_cols = jnp.sum(head_part.astype(jnp.float32), axis=0)
    residual_cols = lax.dynamic_slice_in_dim(
        hidden_in, exp_index * col_width, col_width, 1
    ).astype(jnp.float32) + head_cols
    square_part = jnp.sum(residual_cols * residual_cols, axis=1)
    square_high = square_part.astype(jnp.bfloat16)
    square_low = (square_part - square_high.astype(jnp.float32)).astype(jnp.bfloat16)
    gain_cols = lax.dynamic_slice_in_dim(norm_gain, exp_index * col_width, col_width, 0)
    normed_cols = jnp.concatenate(
        [
            (residual_cols * gain_cols[None, :]).astype(jnp.bfloat16),
            square_high[:, None],
            square_low[:, None],
        ],
        axis=1,
    )
    send_width = col_width + 2
    exp_local = gate_up.shape[0]
    n_experts = exp_local * ctx_count
    top_count = expert_ids.shape[1]
    capacity = max(2, tok_rows * top_count * 5 // (4 * n_experts))
    slot_index = route_slots(expert_ids, n_experts)
    dest_row = expert_ids * capacity + slot_index
    spread_rows = jnp.broadcast_to(
        normed_cols[:, None, :], (tok_rows, top_count, send_width)
    ).reshape(tok_rows * top_count, send_width)
    send_rows = (
        jnp.zeros((n_experts * capacity, send_width), jnp.bfloat16)
        .at[dest_row.reshape(-1)]
        .set(spread_rows)
    )
    bucket_rows = ctx_count * capacity
    unit_count = gate_up.shape[-1]
    received = lax.all_to_all(
        send_rows.reshape(ctx_count, exp_local * capacity, send_width),
        CTX,
        split_axis=0,
        concat_axis=0,
        tiled=True,
    ).reshape(bucket_rows, send_width)
    gathered = lax.all_gather(received, "zll", axis=0, tiled=False)
    gathered = lax.all_gather(gathered, "zlh", axis=0, tiled=False)
    gathered = lax.all_gather(gathered, "c", axis=0, tiled=False)
    gathered = gathered.reshape(c_count, zl_count, bucket_rows, send_width)
    row_squares = jnp.sum(
        gathered[:, :, :, col_width].astype(jnp.float32)
        + gathered[:, :, :, col_width + 1].astype(jnp.float32),
        axis=(0, 1),
    )
    row_scale = lax.rsqrt(row_squares / D + 1e-05)
    weights_flat = gate_up.reshape(zl_count, c_count, col_width, 2 * unit_count)
    gate_up_out = jnp.einsum(
        "czrk,zckf->rf",
        gathered[:, :, :, :col_width],
        weights_flat,
        preferred_element_type=jnp.float32,
    ) * row_scale[:, None]
    gate_up_out = gate_up_out.reshape(bucket_rows, 2, unit_count)
    gate_value = gate_up_out[:, 0]
    up_value = gate_up_out[:, 1]
    activated = ((up_value + 1.0) * gate_value * jax.nn.sigmoid(1.702 * gate_value)).astype(
        jnp.bfloat16
    )
    zlh_count = zl_count // 2
    down_local = down_proj.reshape(unit_count, zlh_count, 2, c_count, col_width)
    partial_value = jnp.einsum(
        "rf,fhlcd->chlrd", activated, down_local, preferred_element_type=jnp.float32
    ).astype(jnp.bfloat16)
    partial_value = lax.all_to_all(partial_value, "c", 0, 0, tiled=True)
    partial_value = jnp.sum(partial_value.astype(jnp.float32), axis=0).astype(jnp.bfloat16)
    partial_value = lax.all_to_all(partial_value.transpose(1, 0, 2, 3), "zll", 0, 0, tiled=True)
    partial_value = jnp.sum(partial_value.astype(jnp.float32), axis=0).astype(jnp.bfloat16)
    partial_value = lax.all_to_all(partial_value, "zlh", 0, 0, tiled=True)
    expert_cols = jnp.sum(partial_value.astype(jnp.float32), axis=0).astype(jnp.bfloat16)
    returned = lax.all_to_all(
        expert_cols.reshape(ctx_count, capacity, col_width),
        CTX,
        split_axis=0,
        concat_axis=0,
        tiled=True,
    )
    picked_rows = returned.reshape(n_experts * capacity, col_width)[dest_row]
    moe_cols = jnp.sum(expert_gates[:, :, None] * picked_rows.astype(jnp.float32), axis=1)
    return (residual_cols + moe_cols).astype(jnp.bfloat16)


def solution(mesh):
    ctx_count, exp_count = mesh.devices.shape
    zh, y, x = (mesh.devices.shape[0] // 16, 4, 4)
    c_count = 2
    zl_count = exp_count // c_count
    fine = Mesh(
        mesh.devices.reshape(zh, y, x, zl_count // 2, 2, c_count), ("zh", "y", "x", "zlh", "zll", "c")
    )
    placed = (
        P(CTX, None),
        P(CTX, EXP),
        P(CTX, None),
        P(CTX, None),
        P(EXP),
        P(EXP, None),
        P(),
        P(CTX, None),
        P(CTX, None),
        P(CTX, None, None, EXP),
        P(CTX, EXP, None),
    )
    return jax.shard_map(
        functools.partial(per_device, ctx_count=ctx_count, zl_count=zl_count, c_count=c_count),
        mesh=fine,
        in_specs=placed,
        out_specs=P(CTX, EXP),
        check_vma=False,
    )
```

```python
import functools
import math

import jax
import jax.numpy as jnp
import numpy as np
from jax import lax
from jax.sharding import Mesh, PartitionSpec as P

D = 2880
QUERY_HEADS = 32
KEY_VALUE_HEADS = 4
HEAD_SIZE = 64


yarn_base = 150000.0
yarn_factor = 32.0
yarn_initial = 4096.0
beta_fast = 32.0
beta_slow = 1.0
neg_large = -1e30


def yarn_frequencies(head_dim):
    half_dim = head_dim // 2

    def correction(rotations):
        return (
            head_dim
            * math.log(yarn_initial / (rotations * 2.0 * math.pi))
            / (2.0 * math.log(yarn_base))
        )

    lower_dim = max(math.floor(correction(beta_fast)), 0)
    upper_dim = min(math.ceil(correction(beta_slow)), head_dim - 1)
    extrap_freq = 1.0 / yarn_base ** (np.arange(0, head_dim, 2) / head_dim)
    interp_freq = extrap_freq / yarn_factor
    ramp_part = np.clip((np.arange(half_dim) - lower_dim) / (upper_dim - lower_dim), 0.0, 1.0)
    extrap_share = 1.0 - ramp_part
    return (interp_freq * (1.0 - extrap_share) + extrap_freq * extrap_share).astype(np.float32)


def rotate_with_yarn(heads_in, token_positions):
    head_dim = heads_in.shape[-1]
    freqs = jnp.asarray(yarn_frequencies(head_dim))
    angles = token_positions.astype(jnp.float32)[:, None] * freqs[None, :]
    factor = 0.1 * math.log(yarn_factor) + 1.0
    cosine = (jnp.cos(angles) * factor)[:, None, :]
    sine = (jnp.sin(angles) * factor)[:, None, :]
    first_half = heads_in[..., : head_dim // 2]
    second_half = heads_in[..., head_dim // 2 :]
    return jnp.concatenate(
        [first_half * cosine - second_half * sine, second_half * cosine + first_half * sine],
        axis=-1,
    )


def route_slots(ids_block, n_experts):
    flat_ids = ids_block.reshape(-1)
    onehot = (flat_ids[:, None] == jnp.arange(n_experts, dtype=jnp.int32)[None, :]).astype(
        jnp.int32
    )
    ranks = jnp.cumsum(onehot, axis=0) - onehot
    return jnp.sum(ranks * onehot, axis=1).reshape(ids_block.shape)


CTX = ("zh", "y", "x")
ZL = ("zlh", "zll")
EXP = ("zlh", "zll", "c")


def per_device(
    hidden_in,
    query_input,
    key_heads_input,
    value_heads_input,
    sink_logits,
    out_proj,
    norm_gain,
    expert_ids,
    expert_gates,
    gate_up,
    down_proj,
    *,
    ctx_count,
    zl_count,
    c_count,
):
    tok_rows = hidden_in.shape[0]
    exp_count = zl_count * c_count
    local_heads = query_input.shape[1] // HEAD_SIZE
    ctx_index = lax.axis_index(CTX)
    exp_index = lax.axis_index(EXP)
    col_width = D // exp_count
    token_positions = ctx_index * tok_rows + jnp.arange(tok_rows, dtype=jnp.int32)
    q_rot = rotate_with_yarn(
        query_input.astype(jnp.float32).reshape(tok_rows, local_heads, HEAD_SIZE), token_positions
    ).astype(jnp.bfloat16)
    shared_key_head = exp_index * local_heads // (QUERY_HEADS // KEY_VALUE_HEADS)
    key_block = lax.dynamic_slice_in_dim(key_heads_input, shared_key_head * HEAD_SIZE, HEAD_SIZE, 1)
    value_block = lax.dynamic_slice_in_dim(
        value_heads_input, shared_key_head * HEAD_SIZE, HEAD_SIZE, 1
    )
    key_rot = (
        rotate_with_yarn(
            key_block.astype(jnp.float32).reshape(tok_rows, 1, HEAD_SIZE), token_positions
        )
        .reshape(tok_rows, HEAD_SIZE)
        .astype(jnp.bfloat16)
    )
    key_value = jnp.concatenate([key_rot, value_block], axis=1)
    score_scale = 1.0 / math.sqrt(HEAD_SIZE)
    block_part = lax.all_gather(key_value, "zh", axis=0, tiled=False)
    block_part = lax.all_to_all(
        jnp.broadcast_to(block_part[None], (lax.axis_size("y"),) + block_part.shape),
        "y",
        0,
        0,
        tiled=True,
    )
    block_part = lax.all_to_all(
        jnp.broadcast_to(block_part[None], (lax.axis_size("x"),) + block_part.shape),
        "x",
        0,
        0,
        tiled=True,
    )
    zh_count = block_part.shape[2]
    y_count = block_part.shape[1]
    x_count = block_part.shape[0]
    block_of_key = (
        lax.broadcasted_iota(jnp.int32, (x_count, y_count, zh_count), 2) * (y_count * x_count)
        + lax.broadcasted_iota(jnp.int32, (x_count, y_count, zh_count), 1) * x_count
        + lax.broadcasted_iota(jnp.int32, (x_count, y_count, zh_count), 0)
    )
    key_pos = (
        block_of_key[:, :, :, None] * tok_rows + jnp.arange(tok_rows, dtype=jnp.int32)
    ).reshape(-1)
    block_part = block_part.reshape(-1, 2 * HEAD_SIZE)
    run_max = jnp.broadcast_to(sink_logits[:, None], (local_heads, tok_rows))
    run_total = jnp.ones((local_heads, tok_rows), jnp.float32)
    key_count = block_part.shape[0]
    key_part = block_part[:, :HEAD_SIZE]
    value_part = block_part[:, HEAD_SIZE:].astype(jnp.float32)
    scores = (
        jnp.einsum("rhd,kd->hrk", q_rot, key_part, preferred_element_type=jnp.float32) * score_scale
    )
    visible = token_positions[:, None] >= key_pos[None, :]
    scores = jnp.where(visible[None, :, :], scores, neg_large)
    new_max = jnp.maximum(run_max, jnp.max(scores, axis=2))
    weights = jnp.exp(scores - new_max[:, :, None])
    factor = jnp.exp(run_max - new_max)
    run_total = run_total * factor + jnp.sum(weights, axis=2)
    run_sum = jnp.einsum("hrk,kd->hrd", weights, value_part, precision=lax.Precision.HIGHEST)
    attended = (
        (run_sum / run_total[:, :, None])
        .transpose(1, 0, 2)
        .reshape(tok_rows, local_heads * HEAD_SIZE)
        .astype(jnp.bfloat16)
    )
    head_part = jnp.dot(attended, out_proj, preferred_element_type=jnp.float32).astype(jnp.bfloat16)
    head_part = head_part.reshape(tok_rows, zl_count, c_count, col_width).transpose(2, 1, 0, 3)
    head_part = lax.all_to_all(head_part, "c", split_axis=0, concat_axis=0, tiled=True)
    head_part = jnp.sum(head_part.astype(jnp.float32), axis=0).astype(jnp.bfloat16)
    head_part = lax.all_to_all(head_part, ZL, split_axis=0, concat_axis=0, tiled=True)
    head_cols = jnp.sum(head_part.astype(jnp.float32), axis=0)
    residual_cols = lax.dynamic_slice_in_dim(
        hidden_in, exp_index * col_width, col_width, 1
    ).astype(jnp.float32) + head_cols
    square_part = jnp.sum(residual_cols * residual_cols, axis=1)
    square_high = square_part.astype(jnp.bfloat16)
    square_low = (square_part - square_high.astype(jnp.float32)).astype(jnp.bfloat16)
    gain_cols = lax.dynamic_slice_in_dim(norm_gain, exp_index * col_width, col_width, 0)
    normed_cols = jnp.concatenate(
        [
            (residual_cols * gain_cols[None, :]).astype(jnp.bfloat16),
            square_high[:, None],
            square_low[:, None],
        ],
        axis=1,
    )
    send_width = col_width + 2
    exp_local = gate_up.shape[0]
    n_experts = exp_local * ctx_count
    top_count = expert_ids.shape[1]
    capacity = max(2, tok_rows * top_count * 5 // (4 * n_experts))
    slot_index = route_slots(expert_ids, n_experts)
    dest_row = expert_ids * capacity + slot_index
    spread_rows = jnp.broadcast_to(
        normed_cols[:, None, :], (tok_rows, top_count, send_width)
    ).reshape(tok_rows * top_count, send_width)
    send_rows = (
        jnp.zeros((n_experts * capacity, send_width), jnp.bfloat16)
        .at[dest_row.reshape(-1)]
        .set(spread_rows)
    )
    bucket_rows = ctx_count * capacity
    unit_count = gate_up.shape[-1]
    received = lax.all_to_all(
        send_rows.reshape(ctx_count, exp_local * capacity, send_width),
        CTX,
        split_axis=0,
        concat_axis=0,
        tiled=True,
    ).reshape(bucket_rows, send_width)
    gathered = lax.all_gather(received, ZL, axis=0, tiled=False)
    gathered = lax.all_gather(gathered, "c", axis=0, tiled=False)
    row_squares = jnp.sum(
        gathered[:, :, :, col_width].astype(jnp.float32)
        + gathered[:, :, :, col_width + 1].astype(jnp.float32),
        axis=(0, 1),
    )
    row_scale = lax.rsqrt(row_squares / D + 1e-05)
    weights_flat = gate_up.reshape(zl_count, c_count, col_width, 2 * unit_count)
    gate_up_out = jnp.einsum(
        "czrk,zckf->rf",
        gathered[:, :, :, :col_width],
        weights_flat,
        preferred_element_type=jnp.float32,
    ) * row_scale[:, None]
    gate_up_out = gate_up_out.reshape(bucket_rows, 2, unit_count)
    gate_value = gate_up_out[:, 0]
    up_value = gate_up_out[:, 1]
    activated = ((up_value + 1.0) * gate_value * jax.nn.sigmoid(1.702 * gate_value)).astype(
        jnp.bfloat16
    )
    zlh_count = zl_count // 2
    down_local = down_proj.reshape(unit_count, zlh_count, 2, c_count, col_width)
    partial_value = jnp.einsum(
        "rf,fhlcd->chlrd", activated, down_local, preferred_element_type=jnp.float32
    ).astype(jnp.bfloat16)
    partial_value = lax.all_to_all(partial_value, "c", 0, 0, tiled=True)
    partial_value = jnp.sum(partial_value.astype(jnp.float32), axis=0).astype(jnp.bfloat16)
    partial_value = lax.all_to_all(partial_value.transpose(1, 0, 2, 3), "zll", 0, 0, tiled=True)
    partial_value = jnp.sum(partial_value.astype(jnp.float32), axis=0).astype(jnp.bfloat16)
    partial_value = lax.all_to_all(partial_value, "zlh", 0, 0, tiled=True)
    expert_cols = jnp.sum(partial_value.astype(jnp.float32), axis=0).astype(jnp.bfloat16)
    returned = lax.all_to_all(
        expert_cols.reshape(ctx_count, capacity, col_width),
        CTX,
        split_axis=0,
        concat_axis=0,
        tiled=True,
    )
    picked_rows = returned.reshape(n_experts * capacity, col_width)[dest_row]
    moe_cols = jnp.sum(expert_gates[:, :, None] * picked_rows.astype(jnp.float32), axis=1)
    return (residual_cols + moe_cols).astype(jnp.bfloat16)


def solution(mesh):
    ctx_count, exp_count = mesh.devices.shape
    zh, y, x = (mesh.devices.shape[0] // 16, 4, 4)
    c_count = 2
    zl_count = exp_count // c_count
    fine = Mesh(
        mesh.devices.reshape(zh, y, x, zl_count // 2, 2, c_count), ("zh", "y", "x", "zlh", "zll", "c")
    )
    placed = (
        P(CTX, None),
        P(CTX, EXP),
        P(CTX, None),
        P(CTX, None),
        P(EXP),
        P(EXP, None),
        P(),
        P(CTX, None),
        P(CTX, None),
        P(CTX, None, None, EXP),
        P(CTX, EXP, None),
    )
    return jax.shard_map(
        functools.partial(per_device, ctx_count=ctx_count, zl_count=zl_count, c_count=c_count),
        mesh=fine,
        in_specs=placed,
        out_specs=P(CTX, EXP),
        check_vma=False,
    )
```

```python
import functools
import math

import jax
import jax.numpy as jnp
import numpy as np
from jax import lax
from jax.sharding import Mesh, PartitionSpec as P

D = 2880
QUERY_HEADS = 32
KEY_VALUE_HEADS = 4
HEAD_SIZE = 64


yarn_base = 150000.0
yarn_factor = 32.0
yarn_initial = 4096.0
beta_fast = 32.0
beta_slow = 1.0
neg_large = -1e30


def yarn_frequencies(head_dim):
    half_dim = head_dim // 2

    def correction(rotations):
        return (
            head_dim
            * math.log(yarn_initial / (rotations * 2.0 * math.pi))
            / (2.0 * math.log(yarn_base))
        )

    lower_dim = max(math.floor(correction(beta_fast)), 0)
    upper_dim = min(math.ceil(correction(beta_slow)), head_dim - 1)
    extrap_freq = 1.0 / yarn_base ** (np.arange(0, head_dim, 2) / head_dim)
    interp_freq = extrap_freq / yarn_factor
    ramp_part = np.clip((np.arange(half_dim) - lower_dim) / (upper_dim - lower_dim), 0.0, 1.0)
    extrap_share = 1.0 - ramp_part
    return (interp_freq * (1.0 - extrap_share) + extrap_freq * extrap_share).astype(np.float32)


def rotate_with_yarn(heads_in, token_positions):
    head_dim = heads_in.shape[-1]
    freqs = jnp.asarray(yarn_frequencies(head_dim))
    angles = token_positions.astype(jnp.float32)[:, None] * freqs[None, :]
    factor = 0.1 * math.log(yarn_factor) + 1.0
    cosine = (jnp.cos(angles) * factor)[:, None, :]
    sine = (jnp.sin(angles) * factor)[:, None, :]
    first_half = heads_in[..., : head_dim // 2]
    second_half = heads_in[..., head_dim // 2 :]
    return jnp.concatenate(
        [first_half * cosine - second_half * sine, second_half * cosine + first_half * sine],
        axis=-1,
    )


def route_slots(ids_block, n_experts):
    flat_ids = ids_block.reshape(-1)
    onehot = (flat_ids[:, None] == jnp.arange(n_experts, dtype=jnp.int32)[None, :]).astype(
        jnp.int32
    )
    ranks = jnp.cumsum(onehot, axis=0) - onehot
    return jnp.sum(ranks * onehot, axis=1).reshape(ids_block.shape)


CTX = ("zh", "y", "x")
ZL = ("zlh", "zll")
EXP = ("zlh", "zll", "c")


def per_device(
    hidden_in,
    query_input,
    key_heads_input,
    value_heads_input,
    sink_logits,
    out_proj,
    norm_gain,
    expert_ids,
    expert_gates,
    gate_up,
    down_proj,
    *,
    ctx_count,
    zl_count,
    c_count,
):
    tok_rows = hidden_in.shape[0]
    exp_count = zl_count * c_count
    local_heads = query_input.shape[1] // HEAD_SIZE
    ctx_index = lax.axis_index(CTX)
    exp_index = lax.axis_index(EXP)
    col_width = D // exp_count
    token_positions = ctx_index * tok_rows + jnp.arange(tok_rows, dtype=jnp.int32)
    q_rot = rotate_with_yarn(
        query_input.astype(jnp.float32).reshape(tok_rows, local_heads, HEAD_SIZE), token_positions
    ).astype(jnp.bfloat16)
    shared_key_head = exp_index * local_heads // (QUERY_HEADS // KEY_VALUE_HEADS)
    key_block = lax.dynamic_slice_in_dim(key_heads_input, shared_key_head * HEAD_SIZE, HEAD_SIZE, 1)
    value_block = lax.dynamic_slice_in_dim(
        value_heads_input, shared_key_head * HEAD_SIZE, HEAD_SIZE, 1
    )
    key_rot = (
        rotate_with_yarn(
            key_block.astype(jnp.float32).reshape(tok_rows, 1, HEAD_SIZE), token_positions
        )
        .reshape(tok_rows, HEAD_SIZE)
        .astype(jnp.bfloat16)
    )
    key_value = jnp.concatenate([key_rot, value_block], axis=1)
    score_scale = 1.0 / math.sqrt(HEAD_SIZE)
    partner_value = lax.ppermute(key_value, "zh", [(0, 1), (1, 0)])
    lower_half = lax.axis_index("zh") == 0
    block_part = jnp.stack(
        [
            jnp.where(lower_half, key_value, partner_value),
            jnp.where(lower_half, partner_value, key_value),
        ]
    )
    block_part = lax.all_to_all(
        jnp.broadcast_to(block_part[None], (lax.axis_size("y"),) + block_part.shape),
        "y",
        0,
        0,
        tiled=True,
    )
    block_part = lax.all_to_all(
        jnp.broadcast_to(block_part[None], (lax.axis_size("x"),) + block_part.shape),
        "x",
        0,
        0,
        tiled=True,
    )
    zh_count = block_part.shape[2]
    y_count = block_part.shape[1]
    x_count = block_part.shape[0]
    block_of_key = (
        lax.broadcasted_iota(jnp.int32, (x_count, y_count, zh_count), 2) * (y_count * x_count)
        + lax.broadcasted_iota(jnp.int32, (x_count, y_count, zh_count), 1) * x_count
        + lax.broadcasted_iota(jnp.int32, (x_count, y_count, zh_count), 0)
    )
    key_pos = (
        block_of_key[:, :, :, None] * tok_rows + jnp.arange(tok_rows, dtype=jnp.int32)
    ).reshape(-1)
    block_part = block_part.reshape(-1, 2 * HEAD_SIZE)
    run_max = jnp.broadcast_to(sink_logits[:, None], (local_heads, tok_rows))
    run_total = jnp.ones((local_heads, tok_rows), jnp.float32)
    key_count = block_part.shape[0]
    key_part = block_part[:, :HEAD_SIZE]
    value_part = block_part[:, HEAD_SIZE:].astype(jnp.float32)
    scores = (
        jnp.einsum("rhd,kd->hrk", q_rot, key_part, preferred_element_type=jnp.float32) * score_scale
    )
    visible = token_positions[:, None] >= key_pos[None, :]
    scores = jnp.where(visible[None, :, :], scores, neg_large)
    new_max = jnp.maximum(run_max, jnp.max(scores, axis=2))
    weights = jnp.exp(scores - new_max[:, :, None])
    factor = jnp.exp(run_max - new_max)
    run_total = run_total * factor + jnp.sum(weights, axis=2)
    run_sum = jnp.einsum("hrk,kd->hrd", weights, value_part, precision=lax.Precision.HIGHEST)
    attended = (
        (run_sum / run_total[:, :, None])
        .transpose(1, 0, 2)
        .reshape(tok_rows, local_heads * HEAD_SIZE)
        .astype(jnp.bfloat16)
    )
    head_part = jnp.dot(attended, out_proj, preferred_element_type=jnp.float32).astype(jnp.bfloat16)
    head_part = head_part.reshape(tok_rows, zl_count, c_count, col_width).transpose(2, 1, 0, 3)
    head_part = lax.all_to_all(head_part, "c", split_axis=0, concat_axis=0, tiled=True)
    head_part = jnp.sum(head_part.astype(jnp.float32), axis=0).astype(jnp.bfloat16)
    head_part = lax.all_to_all(head_part, ZL, split_axis=0, concat_axis=0, tiled=True)
    head_cols = jnp.sum(head_part.astype(jnp.float32), axis=0)
    residual_cols = lax.dynamic_slice_in_dim(
        hidden_in, exp_index * col_width, col_width, 1
    ).astype(jnp.float32) + head_cols
    square_part = jnp.sum(residual_cols * residual_cols, axis=1)
    square_high = square_part.astype(jnp.bfloat16)
    square_low = (square_part - square_high.astype(jnp.float32)).astype(jnp.bfloat16)
    gain_cols = lax.dynamic_slice_in_dim(norm_gain, exp_index * col_width, col_width, 0)
    normed_cols = jnp.concatenate(
        [
            (residual_cols * gain_cols[None, :]).astype(jnp.bfloat16),
            square_high[:, None],
            square_low[:, None],
        ],
        axis=1,
    )
    send_width = col_width + 2
    exp_local = gate_up.shape[0]
    n_experts = exp_local * ctx_count
    top_count = expert_ids.shape[1]
    capacity = max(2, tok_rows * top_count * 5 // (4 * n_experts))
    slot_index = route_slots(expert_ids, n_experts)
    dest_row = expert_ids * capacity + slot_index
    spread_rows = jnp.broadcast_to(
        normed_cols[:, None, :], (tok_rows, top_count, send_width)
    ).reshape(tok_rows * top_count, send_width)
    send_rows = (
        jnp.zeros((n_experts * capacity, send_width), jnp.bfloat16)
        .at[dest_row.reshape(-1)]
        .set(spread_rows)
    )
    bucket_rows = ctx_count * capacity
    unit_count = gate_up.shape[-1]
    received = lax.all_to_all(
        send_rows.reshape(ctx_count, exp_local * capacity, send_width),
        CTX,
        split_axis=0,
        concat_axis=0,
        tiled=True,
    ).reshape(bucket_rows, send_width)
    gathered = lax.all_gather(received, ZL, axis=0, tiled=False)
    gathered = lax.all_gather(gathered, "c", axis=0, tiled=False)
    row_squares = jnp.sum(
        gathered[:, :, :, col_width].astype(jnp.float32)
        + gathered[:, :, :, col_width + 1].astype(jnp.float32),
        axis=(0, 1),
    )
    row_scale = lax.rsqrt(row_squares / D + 1e-05)
    weights_flat = gate_up.reshape(zl_count, c_count, col_width, 2 * unit_count)
    gate_up_out = jnp.einsum(
        "czrk,zckf->rf",
        gathered[:, :, :, :col_width],
        weights_flat,
        preferred_element_type=jnp.float32,
    ) * row_scale[:, None]
    gate_up_out = gate_up_out.reshape(bucket_rows, 2, unit_count)
    gate_value = gate_up_out[:, 0]
    up_value = gate_up_out[:, 1]
    activated = ((up_value + 1.0) * gate_value * jax.nn.sigmoid(1.702 * gate_value)).astype(
        jnp.bfloat16
    )
    zlh_count = zl_count // 2
    down_local = down_proj.reshape(unit_count, zlh_count, 2, c_count, col_width)
    partial_value = jnp.einsum(
        "rf,fhlcd->chlrd", activated, down_local, preferred_element_type=jnp.float32
    ).astype(jnp.bfloat16)
    partial_value = lax.all_to_all(partial_value, "c", 0, 0, tiled=True)
    partial_value = jnp.sum(partial_value.astype(jnp.float32), axis=0).astype(jnp.bfloat16)
    partial_value = lax.all_to_all(partial_value.transpose(1, 0, 2, 3), "zll", 0, 0, tiled=True)
    partial_value = jnp.sum(partial_value.astype(jnp.float32), axis=0).astype(jnp.bfloat16)
    partial_value = lax.all_to_all(partial_value, "zlh", 0, 0, tiled=True)
    expert_cols = jnp.sum(partial_value.astype(jnp.float32), axis=0).astype(jnp.bfloat16)
    returned = lax.all_to_all(
        expert_cols.reshape(ctx_count, capacity, col_width),
        CTX,
        split_axis=0,
        concat_axis=0,
        tiled=True,
    )
    picked_rows = returned.reshape(n_experts * capacity, col_width)[dest_row]
    moe_cols = jnp.sum(expert_gates[:, :, None] * picked_rows.astype(jnp.float32), axis=1)
    return (residual_cols + moe_cols).astype(jnp.bfloat16)


def solution(mesh):
    ctx_count, exp_count = mesh.devices.shape
    zh, y, x = (mesh.devices.shape[0] // 16, 4, 4)
    c_count = 2
    zl_count = exp_count // c_count
    fine = Mesh(
        mesh.devices.reshape(zh, y, x, zl_count // 2, 2, c_count), ("zh", "y", "x", "zlh", "zll", "c")
    )
    placed = (
        P(CTX, None),
        P(CTX, EXP),
        P(CTX, None),
        P(CTX, None),
        P(EXP),
        P(EXP, None),
        P(),
        P(CTX, None),
        P(CTX, None),
        P(CTX, None, None, EXP),
        P(CTX, EXP, None),
    )
    return jax.shard_map(
        functools.partial(per_device, ctx_count=ctx_count, zl_count=zl_count, c_count=c_count),
        mesh=fine,
        in_specs=placed,
        out_specs=P(CTX, EXP),
        check_vma=False,
    )
```
